32 devices in a mesh: parts: 2 (over y), seq: 4 (over z), section: 2 (over x), tp: 2 (over core).
Axes of the slice: x: 2, y: 2, z: 4, core: 2. Of those that a mesh axis runs over, the one named last changes fastest.
Arguments:
- queries: bfloat16 [2, 2048, 4096], P('section', ('parts', 'seq'), 'tp'), parts along dimension 1, may hold values from -82 to 82
- keys_values: bfloat16 [2, 2, 2048, 512], P('section', None, ('parts', 'seq'), 'tp'), parts along dimension 2, may hold values from -4 to 4
- lengths: int32 [2], P('parts'), parts along dimension 0, may hold values from 769 to 1024, as said below
Outputs:
- attended: bfloat16 [2, 2048, 4096], P('section', ('parts', 'seq'), 'tp'), parts along dimension 1
- window_cache: bfloat16 [2, 2, 4096, 512], P('section', None, ('parts', 'seq'), 'tp'), parts along dimension 2
The draws below stay inside these ranges and needn't reach their ends.
There are 2 independent parts, one for each index of `parts`. The reference program is written for one: setup_inputs(seed, part) draws one part's arguments, and reference() takes and returns one part's arrays. A program takes and returns all parts, laid end to end along the dimension named above; each array names one. Nothing has to cross between parts.
Inputs may be any that keep to these rules, and one draw needn't show every extreme that they name: `lengths`: the first request's length lies in min(2048, 1024 - 256) + 1 to min(2048, 1024 - 256) + 256; the second request's length is 1024.
All inputs are finite; a program needn't handle non-finite values.
Results may differ from the reference program's by a relative error of at most 0.0077.
Values may be sent and summed in bfloat16 or wider, within the bound.
No kernel may reach another device: no remote copies, remote signals or barrier semaphores. Data moves between devices by JAX's collectives and lax.ppermute only.
A program may use at most 64 MiB of HBM per device.

```python
import math
import jax
import jax.numpy as jnp
from jax import lax

HEADS = 32
KV_HEADS = 4
HD = 128
WINDOW = 2048
TOK_DEV = 256
TOKENS = 1024
LAYERS = 2


def pair_draw(key):
    base_key = jax.random.fold_in(key, 1234)
    query_key, pair_key = jax.random.split(base_key, 2)
    query_shape = (LAYERS, TOKENS, HEADS, HD)
    pair_shape = (LAYERS, 2, TOKENS, KV_HEADS, HD)
    query_all = 2.5 * jax.random.truncated_normal(query_key, -4.0, 4.0, query_shape, jnp.float32)
    pair_all = jax.random.truncated_normal(pair_key, -4.0, 4.0, pair_shape, jnp.float32)
    return (query_all.reshape(LAYERS, TOKENS, HEADS * HD), pair_all.reshape(LAYERS, 2, TOKENS, KV_HEADS * HD))


def draw_queries(key, part):
    return pair_draw(key)[0].astype(jnp.bfloat16)


def draw_keys_values(key, part):
    return pair_draw(key)[1].astype(jnp.bfloat16)


def draw_lengths(key, part):
    length_key = jax.random.fold_in(key, 4321)
    offset = jax.random.randint(length_key, (1,), 0, TOK_DEV)
    short_len = min(WINDOW, TOKENS - TOK_DEV) + 1 + offset
    full_len = jnp.full((1,), TOKENS, jnp.int32)
    return jnp.where(part == 0, short_len, full_len).astype(jnp.int32)


def setup_inputs(seed: int = 0, part: int = 0) -> dict:
    key_list = jax.random.split(jax.random.key(seed), 4)
    part_keys = jax.random.split(jax.random.fold_in(key_list[3], part), 4)
    return {
        "queries": draw_queries(jax.random.fold_in(jax.random.fold_in(key_list[3], part), 71), part),
        "keys_values": draw_keys_values(jax.random.fold_in(jax.random.fold_in(key_list[3], part), 71), part),
        "lengths": draw_lengths(jax.random.fold_in(jax.random.fold_in(key_list[3], part), 71), part),
    }


rope_base = 1000000.0
neg_floor = -1e+30

def rotate(field, positions):
    half_dim = field.shape[-1] // 2
    frequency = jnp.exp(jnp.arange(half_dim, dtype=jnp.float32) * (-2.0 * math.log(rope_base) / field.shape[-1]))
    angles = positions.astype(jnp.float32)[:, None] * frequency[None, :]
    cosine = jnp.cos(angles)[:, None, :]
    sine_part = jnp.sin(angles)[:, None, :]
    lower_half = field[..., :half_dim]
    upper_half = field[..., half_dim:]
    return jnp.concatenate([lower_half * cosine - upper_half * sine_part, upper_half * cosine + lower_half * sine_part], axis=-1)

def one_layer(layer_queries, layer_pairs, seq_len):
    group_size = HEADS // KV_HEADS
    positions = jnp.arange(TOKENS, dtype=jnp.int32)
    scale = 1.0 / math.sqrt(HD)
    rotated_q = rotate(layer_queries.reshape(TOKENS, HEADS, HD).astype(jnp.float32), positions)
    rotated_q = rotated_q.astype(jnp.bfloat16).reshape(TOKENS, KV_HEADS, group_size, HD)
    rotated_k = rotate(layer_pairs[0].reshape(TOKENS, KV_HEADS, HD).astype(jnp.float32), positions).astype(jnp.bfloat16)
    value_rows = layer_pairs[1].reshape(TOKENS, KV_HEADS, HD)
    query_rows = math.gcd(TOKENS, 512)
    key_span = WINDOW + query_rows
    keys_padded = jnp.concatenate([jnp.zeros((WINDOW, KV_HEADS, HD), jnp.bfloat16), rotated_k], axis=0)
    values_padded = jnp.concatenate([jnp.zeros((WINDOW, KV_HEADS, HD), jnp.bfloat16), value_rows], axis=0)

    def query_block(blk_index):
        begin = (blk_index * query_rows).astype(jnp.int32)
        query_part = lax.dynamic_slice_in_dim(rotated_q, begin, query_rows, 0)
        key_part = lax.dynamic_slice_in_dim(keys_padded, begin, key_span, 0)
        value_part = lax.dynamic_slice_in_dim(values_padded, begin, key_span, 0)
        query_pos = begin + jnp.arange(query_rows, dtype=jnp.int32)
        key_pos = begin - WINDOW + jnp.arange(key_span, dtype=jnp.int32)
        allowed = (key_pos[None, :] <= query_pos[:, None]) & (key_pos[None, :] > query_pos[:, None] - WINDOW)
        allowed = allowed & (key_pos[None, :] >= 0) & (key_pos[None, :] < seq_len)
        scores = jnp.einsum('qkgd,skd->kgqs', query_part.astype(jnp.float32), key_part.astype(jnp.float32)) * scale
        row_top = lax.optimization_barrier(jnp.max(jnp.where(allowed, scores, neg_floor), axis=-1))
        weights = jnp.where(allowed, jnp.exp(scores - row_top[..., None]), 0.0)
        totals = lax.optimization_barrier(jnp.sum(weights, axis=-1))
        rounded_weights = weights.astype(jnp.bfloat16)
        numer = jnp.einsum('kgqs,skd->qkgd', rounded_weights.astype(jnp.float32), value_part.astype(jnp.float32))
        valid = query_pos < seq_len
        denom = jnp.where(valid[:, None, None], jnp.moveaxis(totals, 2, 0), 1.0)
        result = jnp.where(valid[:, None, None, None], numer / denom[..., None], 0.0)
        return result.astype(jnp.bfloat16).reshape(query_rows, HEADS * HD)
    attended = lax.map(query_block, jnp.arange(TOKENS // query_rows, dtype=jnp.int32)).reshape(TOKENS, HEADS * HD)
    slots = jnp.arange(WINDOW, dtype=jnp.int32)
    source_pos = seq_len - WINDOW + slots
    is_live = source_pos >= 0
    source_row = jnp.clip(source_pos, 0, TOKENS - 1).astype(jnp.int32)
    key_cache = jnp.where(is_live[:, None], jnp.take(rotated_k.reshape(TOKENS, KV_HEADS * HD), source_row, axis=0), jnp.zeros((), jnp.bfloat16))
    value_cache = jnp.where(is_live[:, None], jnp.take(layer_pairs[1], source_row, axis=0), jnp.zeros((), jnp.bfloat16))
    window_cache = jnp.stack([key_cache, value_cache]).astype(jnp.bfloat16)
    return (attended, window_cache)

def reference(queries, keys_values, lengths):
    seq_len = lengths[0].astype(jnp.int32)
    attended, window_cache = lax.map(lambda pair: one_layer(pair[0], pair[1], seq_len), (queries, keys_values))
    return (attended, window_cache)
```

```python
import functools
import math

import jax
import jax.numpy as jnp
from jax import lax
from jax.experimental import pallas as pl
from jax.experimental.pallas import tpu as pltpu
from jax.sharding import PartitionSpec as P

HD = 128
WINDOW = 2048


rope_base = 1000000.0
neg_floor = -1e30


def rotate(field, positions):
    half_dim = field.shape[-1] // 2
    frequency = jnp.exp(
        jnp.arange(half_dim, dtype=jnp.float32) * (-2.0 * math.log(rope_base) / field.shape[-1])
    )
    angles = positions.astype(jnp.float32)[:, None] * frequency[None, :]
    cosine = jnp.cos(angles)[:, None, :]
    sine_part = jnp.sin(angles)[:, None, :]
    lower_half = field[..., :half_dim]
    upper_half = field[..., half_dim:]
    return jnp.concatenate(
        [
            lower_half * cosine - upper_half * sine_part,
            upper_half * cosine + lower_half * sine_part,
        ],
        axis=-1,
    )


def attend_kernel(scalars, q_ref, k_ref, v_ref, o_ref, *, rows, span):
    seq_len = scalars[0]
    first_pos = scalars[1]
    key_start = pl.multiple_of(scalars[2], 256)
    q = q_ref[...]
    k = k_ref[0, pl.ds(key_start, span), :]
    v = v_ref[0, pl.ds(key_start, span), :]
    scores = lax.dot_general(
        q, k, (((1,), (1,)), ((), ())), preferred_element_type=jnp.float32
    ) * (1.0 / math.sqrt(HD))
    query_pos = first_pos + lax.broadcasted_iota(jnp.int32, (rows, span), 0)
    key_pos = key_start + lax.broadcasted_iota(jnp.int32, (rows, span), 1)
    allowed = (key_pos <= query_pos) & (key_pos > query_pos - WINDOW) & (key_pos < seq_len)
    row_top = jnp.max(jnp.where(allowed, scores, neg_floor), axis=-1, keepdims=True)
    weights = jnp.where(allowed, jnp.exp(scores - row_top), 0.0)
    totals = jnp.sum(weights, axis=-1, keepdims=True)
    numer = jnp.dot(weights.astype(jnp.bfloat16), v, preferred_element_type=jnp.float32)
    valid = (first_pos + lax.broadcasted_iota(jnp.int32, (rows, 1), 0)) < seq_len
    denom = jnp.where(valid, totals, 1.0)
    o_ref[...] = jnp.where(valid, numer / denom, 0.0).astype(o_ref.dtype)


def attention(scalars, rotated_q, gathered, heads_dev, group_size, span):
    rows = rotated_q.shape[0]
    tokens = gathered.shape[1]
    kernel = functools.partial(attend_kernel, rows=rows, span=span)
    grid_spec = pltpu.PrefetchScalarGridSpec(
        num_scalar_prefetch=1,
        grid=(heads_dev,),
        in_specs=[
            pl.BlockSpec((rows, HD), lambda h, s: (0, h)),
            pl.BlockSpec((1, tokens, HD), lambda h, s: (0, 0, h // group_size)),
            pl.BlockSpec((1, tokens, HD), lambda h, s: (1, 0, h // group_size)),
        ],
        out_specs=pl.BlockSpec((rows, HD), lambda h, s: (0, h)),
    )
    return pl.pallas_call(
        kernel,
        grid_spec=grid_spec,
        out_shape=jax.ShapeDtypeStruct((rows, heads_dev * HD), jnp.bfloat16),
    )(scalars, rotated_q, gathered, gathered)


def local(queries, keys_values, lengths):
    seq_len = lengths[0]
    shard_rows = queries.shape[1]
    width = keys_values.shape[-1]
    kv_heads_dev = width // HD
    heads_dev = queries.shape[-1] // HD
    group_size = heads_dev // kv_heads_dev
    seq_index = lax.axis_index("seq")
    seq_count = lax.axis_size("seq")
    first_pos = seq_index * shard_rows
    positions = first_pos + jnp.arange(shard_rows, dtype=jnp.int32)
    rotated_q = rotate(queries[0].reshape(shard_rows, heads_dev, HD).astype(jnp.float32), positions)
    rotated_q = rotated_q.astype(jnp.bfloat16).reshape(shard_rows, heads_dev * HD)
    rotated_k = rotate(
        keys_values[0, 0].reshape(shard_rows, kv_heads_dev, HD).astype(jnp.float32), positions
    )
    own_block = jnp.stack(
        [rotated_k.astype(jnp.bfloat16).reshape(shard_rows, width), keys_values[0, 1]]
    )
    gathered = lax.all_gather(own_block, "seq", axis=1, tiled=True)
    tokens = gathered.shape[1]

    reach_count = min(WINDOW // shard_rows, seq_count - 1)
    span = (reach_count + 1) * shard_rows
    key_start = jnp.maximum(first_pos - reach_count * shard_rows, 0)
    scalars = jnp.stack([seq_len, first_pos, key_start]).astype(jnp.int32)
    attended = attention(scalars, rotated_q, gathered, heads_dev, group_size, span)
    attended = attended.reshape(1, shard_rows, heads_dev * HD)

    slot_rows = WINDOW // seq_count
    padded = jnp.concatenate([jnp.zeros((2, WINDOW, width), jnp.bfloat16), gathered], axis=1)
    begin_row = seq_len + seq_index * slot_rows
    window_cache = lax.dynamic_slice_in_dim(padded, begin_row, slot_rows, 1)
    del tokens
    return (attended, window_cache[None])


def solution(mesh):
    return jax.shard_map(
        local,
        mesh=mesh,
        in_specs=(
            P("section", ("parts", "seq"), "tp"),
            P("section", None, ("parts", "seq"), "tp"),
            P("parts"),
        ),
        out_specs=(
            P("section", ("parts", "seq"), "tp"),
            P("section", None, ("parts", "seq"), "tp"),
        ),
        check_vma=False,
    )
```

```python
import functools
import math

import jax
import jax.numpy as jnp
from jax import lax
from jax.experimental import pallas as pl
from jax.experimental.pallas import tpu as pltpu
from jax.sharding import PartitionSpec as P

HD = 128
WINDOW = 2048


rope_base = 1000000.0
neg_floor = -1e30


def rotate(field, positions):
    half_dim = field.shape[-1] // 2
    frequency = jnp.exp(
        jnp.arange(half_dim, dtype=jnp.float32) * (-2.0 * math.log(rope_base) / field.shape[-1])
    )
    angles = positions.astype(jnp.float32)[:, None] * frequency[None, :]
    cosine = jnp.cos(angles)[:, None, :]
    sine_part = jnp.sin(angles)[:, None, :]
    lower_half = field[..., :half_dim]
    upper_half = field[..., half_dim:]
    return jnp.concatenate(
        [
            lower_half * cosine - upper_half * sine_part,
            upper_half * cosine + lower_half * sine_part,
        ],
        axis=-1,
    )


def attend_kernel(scalars, q_ref, k_ref, v_ref, o_ref, *, rows, span):
    seq_len = scalars[0]
    first_pos = scalars[1]
    key_start = pl.multiple_of(scalars[2], 256)
    q = q_ref[...]
    k = k_ref[0, pl.ds(key_start, span), :]
    v = v_ref[0, pl.ds(key_start, span), :]
    scores = lax.dot_general(
        q, k, (((1,), (1,)), ((), ())), preferred_element_type=jnp.float32
    ) * (1.0 / math.sqrt(HD))
    query_pos = first_pos + lax.broadcasted_iota(jnp.int32, (rows, span), 0)
    key_pos = key_start + lax.broadcasted_iota(jnp.int32, (rows, span), 1)
    allowed = (key_pos <= query_pos) & (key_pos > query_pos - WINDOW) & (key_pos < seq_len)
    row_top = jnp.max(jnp.where(allowed, scores, neg_floor), axis=-1, keepdims=True)
    weights = jnp.where(allowed, jnp.exp(scores - row_top), 0.0)
    totals = jnp.sum(weights, axis=-1, keepdims=True)
    numer = jnp.dot(weights.astype(jnp.bfloat16), v, preferred_element_type=jnp.float32)
    valid = (first_pos + lax.broadcasted_iota(jnp.int32, (rows, 1), 0)) < seq_len
    denom = jnp.where(valid, totals, 1.0)
    o_ref[...] = jnp.where(valid, numer / denom, 0.0).astype(o_ref.dtype)


def attention(scalars, rotated_q, gathered, heads_dev, group_size, span):
    rows = rotated_q.shape[0]
    tokens = gathered.shape[1]
    kernel = functools.partial(attend_kernel, rows=rows, span=span)
    grid_spec = pltpu.PrefetchScalarGridSpec(
        num_scalar_prefetch=1,
        grid=(heads_dev,),
        in_specs=[
            pl.BlockSpec((rows, HD), lambda h, s: (0, h)),
            pl.BlockSpec((1, tokens, HD), lambda h, s: (0, 0, h // group_size)),
            pl.BlockSpec((1, tokens, HD), lambda h, s: (1, 0, h // group_size)),
        ],
        out_specs=pl.BlockSpec((rows, HD), lambda h, s: (0, h)),
    )
    return pl.pallas_call(
        kernel,
        grid_spec=grid_spec,
        out_shape=jax.ShapeDtypeStruct((rows, heads_dev * HD), jnp.bfloat16),
    )(scalars, rotated_q, gathered, gathered)


def local(queries, keys_values, lengths):
    seq_len = lengths[0]
    shard_rows = queries.shape[1]
    width = keys_values.shape[-1]
    kv_heads_dev = width // HD
    heads_dev = queries.shape[-1] // HD
    group_size = heads_dev // kv_heads_dev
    seq_index = lax.axis_index("seq")
    seq_count = lax.axis_size("seq")
    first_pos = seq_index * shard_rows
    positions = first_pos + jnp.arange(shard_rows, dtype=jnp.int32)
    rotated_q = rotate(queries[0].reshape(shard_rows, heads_dev, HD).astype(jnp.float32), positions)
    rotated_q = rotated_q.astype(jnp.bfloat16).reshape(shard_rows, heads_dev * HD)
    rotated_k = rotate(
        keys_values[0, 0].reshape(shard_rows, kv_heads_dev, HD).astype(jnp.float32), positions
    )
    own_block = jnp.stack(
        [rotated_k.astype(jnp.bfloat16).reshape(shard_rows, width), keys_values[0, 1]]
    )
    outbox = jnp.broadcast_to(own_block[:, None], (2, seq_count, shard_rows, width))
    gathered = lax.all_to_all(
        outbox.reshape(2, seq_count * shard_rows, width), "seq", 1, 1, tiled=True
    )
    tokens = gathered.shape[1]

    reach_count = min(WINDOW // shard_rows, seq_count - 1)
    span = (reach_count + 1) * shard_rows
    key_start = jnp.maximum(first_pos - reach_count * shard_rows, 0)
    scalars = jnp.stack([seq_len, first_pos, key_start]).astype(jnp.int32)
    attended = attention(scalars, rotated_q, gathered, heads_dev, group_size, span)
    attended = attended.reshape(1, shard_rows, heads_dev * HD)

    slot_rows = WINDOW // seq_count
    padded = jnp.concatenate([jnp.zeros((2, WINDOW, width), jnp.bfloat16), gathered], axis=1)
    begin_row = seq_len + seq_index * slot_rows
    window_cache = lax.dynamic_slice_in_dim(padded, begin_row, slot_rows, 1)
    del tokens
    return (attended, window_cache[None])


def solution(mesh):
    return jax.shard_map(
        local,
        mesh=mesh,
        in_specs=(
            P("section", ("parts", "seq"), "tp"),
            P("section", None, ("parts", "seq"), "tp"),
            P("parts"),
        ),
        out_specs=(
            P("section", ("parts", "seq"), "tp"),
            P("section", None, ("parts", "seq"), "tp"),
        ),
        check_vma=False,
    )
```

```python
import functools
import math

import jax
import jax.numpy as jnp
from jax import lax
from jax.experimental import pallas as pl
from jax.experimental.pallas import tpu as pltpu
from jax.sharding import PartitionSpec as P

HD = 128
WINDOW = 2048


rope_base = 1000000.0
neg_floor = -1e30


def rotate(field, positions):
    half_dim = field.shape[-1] // 2
    frequency = jnp.exp(
        jnp.arange(half_dim, dtype=jnp.float32) * (-2.0 * math.log(rope_base) / field.shape[-1])
    )
    angles = positions.astype(jnp.float32)[:, None] * frequency[None, :]
    cosine = jnp.cos(angles)[:, None, :]
    sine_part = jnp.sin(angles)[:, None, :]
    lower_half = field[..., :half_dim]
    upper_half = field[..., half_dim:]
    return jnp.concatenate(
        [
            lower_half * cosine - upper_half * sine_part,
            upper_half * cosine + lower_half * sine_part,
        ],
        axis=-1,
    )


def attend_kernel(scalars, q_ref, k_ref, v_ref, o_ref, bias_ref, *, rows, span, group):
    seq_len = scalars[0]
    first_pos = scalars[1]
    key_start = pl.multiple_of(scalars[2], 256)
    query_pos = first_pos + lax.broadcasted_iota(jnp.int32, (rows, span), 0)
    key_pos = key_start + lax.broadcasted_iota(jnp.int32, (rows, span), 1)
    allowed = (key_pos <= query_pos) & (key_pos > query_pos - WINDOW) & (key_pos < seq_len)
    bias_ref[...] = jnp.where(allowed, 0.0, neg_floor)
    k = k_ref[0, pl.ds(key_start, span), :]
    v = v_ref[0, pl.ds(key_start, span), :]
    valid = (first_pos + lax.broadcasted_iota(jnp.int32, (rows, 1), 0)) < seq_len
    scale = 1.0 / math.sqrt(HD)
    for head in range(group):
        cols = slice(head * HD, (head + 1) * HD)
        raw = lax.dot_general(
            q_ref[:, cols], k, (((1,), (1,)), ((), ())), preferred_element_type=jnp.float32
        ) + bias_ref[...]
        row_top = jnp.max(raw, axis=-1, keepdims=True)
        weights = jnp.exp((raw - row_top) * scale)
        totals = jnp.sum(weights, axis=-1, keepdims=True)
        numer = jnp.dot(weights.astype(jnp.bfloat16), v, preferred_element_type=jnp.float32)
        denom = jnp.where(valid, totals, 1.0)
        o_ref[:, cols] = jnp.where(valid, numer / denom, 0.0).astype(o_ref.dtype)


def attention(scalars, rotated_q, gathered, kv_heads_dev, group_size, span):
    rows = rotated_q.shape[0]
    tokens = gathered.shape[1]
    kernel = functools.partial(attend_kernel, rows=rows, span=span, group=group_size)
    width = group_size * HD
    grid_spec = pltpu.PrefetchScalarGridSpec(
        num_scalar_prefetch=1,
        grid=(kv_heads_dev,),
        in_specs=[
            pl.BlockSpec((rows, width), lambda j, s: (0, j)),
            pl.BlockSpec((1, tokens, HD), lambda j, s: (0, 0, j)),
            pl.BlockSpec((1, tokens, HD), lambda j, s: (1, 0, j)),
        ],
        out_specs=pl.BlockSpec((rows, width), lambda j, s: (0, j)),
        scratch_shapes=[pltpu.VMEM((rows, span), jnp.float32)],
    )
    return pl.pallas_call(
        kernel,
        grid_spec=grid_spec,
        out_shape=jax.ShapeDtypeStruct((rows, kv_heads_dev * width), jnp.bfloat16),
    )(scalars, rotated_q, gathered, gathered)


def local(queries, keys_values, lengths):
    seq_len = lengths[0]
    shard_rows = queries.shape[1]
    width = keys_values.shape[-1]
    kv_heads_dev = width // HD
    heads_dev = queries.shape[-1] // HD
    group_size = heads_dev // kv_heads_dev
    seq_index = lax.axis_index("seq")
    seq_count = lax.axis_size("seq")
    first_pos = seq_index * shard_rows
    positions = first_pos + jnp.arange(shard_rows, dtype=jnp.int32)
    rotated_q = rotate(queries[0].reshape(shard_rows, heads_dev, HD).astype(jnp.float32), positions)
    rotated_q = rotated_q.astype(jnp.bfloat16).reshape(shard_rows, heads_dev * HD)
    rotated_k = rotate(
        keys_values[0, 0].reshape(shard_rows, kv_heads_dev, HD).astype(jnp.float32), positions
    )
    own_block = jnp.stack(
        [rotated_k.astype(jnp.bfloat16).reshape(shard_rows, width), keys_values[0, 1]]
    )
    outbox = jnp.broadcast_to(own_block[:, None], (2, seq_count, shard_rows, width))
    gathered = lax.all_to_all(
        outbox.reshape(2, seq_count * shard_rows, width), "seq", 1, 1, tiled=True
    )
    tokens = gathered.shape[1]

    reach_count = min(WINDOW // shard_rows, seq_count - 1)
    span = (reach_count + 1) * shard_rows
    key_start = jnp.maximum(first_pos - reach_count * shard_rows, 0)
    scalars = jnp.stack([seq_len, first_pos, key_start]).astype(jnp.int32)
    attended = attention(scalars, rotated_q, gathered, kv_heads_dev, group_size, span)
    attended = attended.reshape(1, shard_rows, heads_dev * HD)

    slot_rows = WINDOW // seq_count
    padded = jnp.concatenate([jnp.zeros((2, WINDOW, width), jnp.bfloat16), gathered], axis=1)
    begin_row = seq_len + seq_index * slot_rows
    window_cache = lax.dynamic_slice_in_dim(padded, begin_row, slot_rows, 1)
    del tokens
    return (attended, window_cache[None])


def solution(mesh):
    return jax.shard_map(
        local,
        mesh=mesh,
        in_specs=(
            P("section", ("parts", "seq"), "tp"),
            P("section", None, ("parts", "seq"), "tp"),
            P("parts"),
        ),
        out_specs=(
            P("section", ("parts", "seq"), "tp"),
            P("section", None, ("parts", "seq"), "tp"),
        ),
        check_vma=False,
    )
```

```python
import functools
import math

import jax
import jax.numpy as jnp
from jax import lax
from jax.experimental import pallas as pl
from jax.experimental.pallas import tpu as pltpu
from jax.sharding import PartitionSpec as P

HD = 128
WINDOW = 2048


rope_base = 1000000.0
neg_floor = -1e30


def rotate(field, positions):
    half_dim = field.shape[-1] // 2
    frequency = jnp.exp(
        jnp.arange(half_dim, dtype=jnp.float32) * (-2.0 * math.log(rope_base) / field.shape[-1])
    )
    angles = positions.astype(jnp.float32)[:, None] * frequency[None, :]
    cosine = jnp.cos(angles)[:, None, :]
    sine_part = jnp.sin(angles)[:, None, :]
    lower_half = field[..., :half_dim]
    upper_half = field[..., half_dim:]
    return jnp.concatenate(
        [
            lower_half * cosine - upper_half * sine_part,
            upper_half * cosine + lower_half * sine_part,
        ],
        axis=-1,
    )


def attend_kernel(scalars, q_ref, *refs, nblk, rows, group, init, final):
    kv_refs = refs[:nblk]
    refs = refs[nblk:]
    if not init:
        m_in, l_in, acc_in = refs[:3]
        refs = refs[3:]
    if final:
        o_ref, bias_ref = refs
    else:
        m_out, l_out, acc_out, bias_ref = refs
    seq_len = scalars[0]
    first_pos = scalars[1]
    key_first = scalars[2]
    blk = kv_refs[0].shape[1]
    span = nblk * blk
    query_pos = first_pos + lax.broadcasted_iota(jnp.int32, (rows, span), 0)
    key_pos = key_first + lax.broadcasted_iota(jnp.int32, (rows, span), 1)
    allowed = (
        (key_pos <= query_pos)
        & (key_pos > query_pos - WINDOW)
        & (key_pos >= 0)
        & (key_pos < seq_len)
    )
    bias_ref[...] = jnp.where(allowed, 0.0, neg_floor)
    valid = (first_pos + lax.broadcasted_iota(jnp.int32, (rows, 1), 0)) < seq_len
    scale = 1.0 / math.sqrt(HD)
    for head in range(group):
        cols = slice(head * HD, (head + 1) * HD)
        q = q_ref[:, cols]
        raws = [
            lax.dot_general(
                q, kv_refs[b][0], (((1,), (1,)), ((), ())), preferred_element_type=jnp.float32
            )
            + bias_ref[:, b * blk:(b + 1) * blk]
            for b in range(nblk)
        ]
        top = functools.reduce(
            jnp.maximum, [jnp.max(r, axis=-1, keepdims=True) for r in raws]
        )
        if not init:
            top_old = m_in[0, :, head:head + 1]
            top = jnp.maximum(top, top_old)
        weights = [jnp.exp((r - top) * scale) for r in raws]
        totals = functools.reduce(
            jnp.add, [jnp.sum(w, axis=-1, keepdims=True) for w in weights]
        )
        numer = functools.reduce(
            jnp.add,
            [
                jnp.dot(w.astype(jnp.bfloat16), kv_refs[b][1], preferred_element_type=jnp.float32)
                for b, w in enumerate(weights)
            ],
        )
        if not init:
            rescale = jnp.exp((top_old - top) * scale)
            totals = l_in[0, :, head:head + 1] * rescale + totals
            numer = acc_in[:, cols] * rescale + numer
        if final:
            denom = jnp.where(valid, totals, 1.0)
            o_ref[:, cols] = jnp.where(valid, numer / denom, 0.0).astype(o_ref.dtype)
        else:
            m_out[0, :, head:head + 1] = top
            l_out[0, :, head:head + 1] = totals
            acc_out[:, cols] = numer


def attend(scalars, rotated_q, blocks, state, kv_heads_dev, group_size, final):
    rows = rotated_q.shape[0]
    nblk = len(blocks)
    blk = blocks[0].shape[1]
    width = group_size * HD
    init = state is None
    kernel = functools.partial(
        attend_kernel, nblk=nblk, rows=rows, group=group_size, init=init, final=final
    )
    acc_spec = pl.BlockSpec((rows, width), lambda j, s: (0, j))
    top_spec = pl.BlockSpec((1, rows, group_size), lambda j, s: (j, 0, 0))
    in_specs = [acc_spec] + [pl.BlockSpec((2, blk, HD), lambda j, s: (0, 0, j))] * nblk
    operands = [rotated_q] + list(blocks)
    if not init:
        in_specs += [top_spec, top_spec, acc_spec]
        operands += list(state)
    top_shape = jax.ShapeDtypeStruct((kv_heads_dev, rows, group_size), jnp.float32)
    if final:
        out_specs = acc_spec
        out_shape = jax.ShapeDtypeStruct((rows, kv_heads_dev * width), jnp.bfloat16)
    else:
        out_specs = [top_spec, top_spec, acc_spec]
        out_shape = [
            top_shape,
            top_shape,
            jax.ShapeDtypeStruct((rows, kv_heads_dev * width), jnp.float32),
        ]
    grid_spec = pltpu.PrefetchScalarGridSpec(
        num_scalar_prefetch=1,
        grid=(kv_heads_dev,),
        in_specs=in_specs,
        out_specs=out_specs,
        scratch_shapes=[pltpu.VMEM((rows, nblk * blk), jnp.float32)],
    )
    return pl.pallas_call(kernel, grid_spec=grid_spec, out_shape=out_shape)(
        scalars, *operands
    )


def passed_along(x, by):
    devices = lax.axis_size("seq")
    pairs = [(i, i + by) for i in range(devices) if 0 <= i + by < devices]
    return lax.ppermute(x, "seq", pairs)


def local(queries, keys_values, lengths):
    seq_len = lengths[0]
    shard_rows = queries.shape[1]
    width = keys_values.shape[-1]
    kv_heads_dev = width // HD
    heads_dev = queries.shape[-1] // HD
    group_size = heads_dev // kv_heads_dev
    seq_index = lax.axis_index("seq")
    seq_count = lax.axis_size("seq")
    tokens = seq_count * shard_rows
    first_pos = seq_index * shard_rows
    positions = first_pos + jnp.arange(shard_rows, dtype=jnp.int32)
    rotated_k = rotate(
        keys_values[0, 0].reshape(shard_rows, kv_heads_dev, HD).astype(jnp.float32), positions
    )
    own_block = jnp.stack(
        [rotated_k.astype(jnp.bfloat16).reshape(shard_rows, width), keys_values[0, 1]]
    )
    reach_count = min(WINDOW // shard_rows, seq_count - 1)
    slot_rows = WINDOW // seq_count
    if WINDOW >= tokens:
        older = []
        moving = own_block
        for hop in range(reach_count):
            moving = passed_along(moving, 1)
            older.append(moving)
        tail = jnp.concatenate(older[::-1] + [own_block], axis=1)
        tail_first = first_pos - reach_count * shard_rows
    else:
        outbox = jnp.broadcast_to(own_block[:, None], (2, seq_count, shard_rows, width))
        tail = lax.all_to_all(
            outbox.reshape(2, tokens, width), "seq", 1, 1, tiled=True
        )
        tail_first = 0
        older = [
            lax.dynamic_slice_in_dim(
                tail, jnp.maximum(seq_index - hop - 1, 0) * shard_rows, shard_rows, 1
            )
            for hop in range(reach_count)
        ]
    rotated_q = rotate(queries[0].reshape(shard_rows, heads_dev, HD).astype(jnp.float32), positions)
    rotated_q = rotated_q.astype(jnp.bfloat16).reshape(shard_rows, heads_dev * HD)

    def scalars_for(first_key):
        return jnp.stack([seq_len, first_pos, first_key]).astype(jnp.int32)

    near = [older[0], own_block] if reach_count >= 1 else [own_block]
    far = older[1:][::-1]
    near_first = first_pos - (len(near) - 1) * shard_rows
    if far:
        state = attend(scalars_for(near_first), rotated_q, near, None, kv_heads_dev, group_size, False)
        far_first = first_pos - reach_count * shard_rows
        attended = attend(
            scalars_for(far_first), rotated_q, far, state, kv_heads_dev, group_size, True
        )
    else:
        attended = attend(scalars_for(near_first), rotated_q, near, None, kv_heads_dev, group_size, True)
    attended = attended.reshape(1, shard_rows, heads_dev * HD)

    padded = jnp.concatenate([jnp.zeros((2, WINDOW, width), jnp.bfloat16), tail], axis=1)
    begin_row = seq_len - tail_first + seq_index * slot_rows
    window_cache = lax.dynamic_slice_in_dim(padded, begin_row, slot_rows, 1)
    return (attended, window_cache[None])


def solution(mesh):
    return jax.shard_map(
        local,
        mesh=mesh,
        in_specs=(
            P("section", ("parts", "seq"), "tp"),
            P("section", None, ("parts", "seq"), "tp"),
            P("parts"),
        ),
        out_specs=(
            P("section", ("parts", "seq"), "tp"),
            P("section", None, ("parts", "seq"), "tp"),
        ),
        check_vma=False,
    )
```

```python
import functools
import math

import jax
import jax.numpy as jnp
from jax import lax
from jax.experimental import pallas as pl
from jax.experimental.pallas import tpu as pltpu
from jax.sharding import PartitionSpec as P

HD = 128
WINDOW = 2048


rope_base = 1000000.0
neg_floor = -1e30


def rotate(field, positions):
    half_dim = field.shape[-1] // 2
    frequency = jnp.exp(
        jnp.arange(half_dim, dtype=jnp.float32) * (-2.0 * math.log(rope_base) / field.shape[-1])
    )
    angles = positions.astype(jnp.float32)[:, None] * frequency[None, :]
    cosine = jnp.cos(angles)[:, None, :]
    sine_part = jnp.sin(angles)[:, None, :]
    lower_half = field[..., :half_dim]
    upper_half = field[..., half_dim:]
    return jnp.concatenate(
        [
            lower_half * cosine - upper_half * sine_part,
            upper_half * cosine + lower_half * sine_part,
        ],
        axis=-1,
    )


def attend_kernel(scalars, q_ref, k_ref, v_ref, o_ref, bias_ref, raw_ref, w_ref, tot_ref,
                  *, rows, span, group, chunk):
    seq_len = scalars[0]
    first_pos = scalars[1]
    key_start = pl.multiple_of(scalars[2], 256)
    query_pos = first_pos + lax.broadcasted_iota(jnp.int32, (rows, span), 0)
    key_pos = key_start + lax.broadcasted_iota(jnp.int32, (rows, span), 1)
    allowed = (key_pos <= query_pos) & (key_pos > query_pos - WINDOW) & (key_pos < seq_len)
    bias_ref[...] = jnp.where(allowed, 0.0, neg_floor)
    k = k_ref[0, pl.ds(key_start, span), :]
    v = v_ref[0, pl.ds(key_start, span), :]
    valid = (first_pos + lax.broadcasted_iota(jnp.int32, (rows, 1), 0)) < seq_len
    scale = 1.0 / math.sqrt(HD)

    def softmax_rows(c, carry):
        r0 = pl.multiple_of(c * chunk, chunk)
        x = raw_ref[pl.ds(r0, chunk), :] + bias_ref[pl.ds(r0, chunk), :]
        top = jnp.max(x, axis=-1, keepdims=True)
        weights = jnp.exp((x - top) * scale)
        tot_ref[pl.ds(r0, chunk), :] = jnp.sum(weights, axis=-1, keepdims=True)
        w_ref[pl.ds(r0, chunk), :] = weights.astype(jnp.bfloat16)
        return carry

    for head in range(group):
        cols = slice(head * HD, (head + 1) * HD)
        raw_ref[...] = lax.dot_general(
            q_ref[:, cols], k, (((1,), (1,)), ((), ())), preferred_element_type=jnp.float32
        )
        lax.fori_loop(0, rows // chunk, softmax_rows, 0)
        numer = jnp.dot(w_ref[...], v, preferred_element_type=jnp.float32)
        denom = jnp.where(valid, tot_ref[...], 1.0)
        o_ref[:, cols] = jnp.where(valid, numer / denom, 0.0).astype(o_ref.dtype)


def attention(scalars, rotated_q, gathered, kv_heads_dev, group_size, span):
    rows = rotated_q.shape[0]
    tokens = gathered.shape[1]
    chunk = 32 if span <= 1024 else 16
    kernel = functools.partial(
        attend_kernel, rows=rows, span=span, group=group_size, chunk=chunk
    )
    width = group_size * HD
    grid_spec = pltpu.PrefetchScalarGridSpec(
        num_scalar_prefetch=1,
        grid=(kv_heads_dev,),
        in_specs=[
            pl.BlockSpec((rows, width), lambda j, s: (0, j)),
            pl.BlockSpec((1, tokens, HD), lambda j, s: (0, 0, j)),
            pl.BlockSpec((1, tokens, HD), lambda j, s: (1, 0, j)),
        ],
        out_specs=pl.BlockSpec((rows, width), lambda j, s: (0, j)),
        scratch_shapes=[
            pltpu.VMEM((rows, span), jnp.float32),
            pltpu.VMEM((rows, span), jnp.float32),
            pltpu.VMEM((rows, span), jnp.bfloat16),
            pltpu.VMEM((rows, 1), jnp.float32),
        ],
    )
    return pl.pallas_call(
        kernel,
        grid_spec=grid_spec,
        out_shape=jax.ShapeDtypeStruct((rows, kv_heads_dev * width), jnp.bfloat16),
    )(scalars, rotated_q, gathered, gathered)


def local(queries, keys_values, lengths):
    seq_len = lengths[0]
    shard_rows = queries.shape[1]
    width = keys_values.shape[-1]
    kv_heads_dev = width // HD
    heads_dev = queries.shape[-1] // HD
    group_size = heads_dev // kv_heads_dev
    seq_index = lax.axis_index("seq")
    seq_count = lax.axis_size("seq")
    first_pos = seq_index * shard_rows
    positions = first_pos + jnp.arange(shard_rows, dtype=jnp.int32)
    rotated_q = rotate(queries[0].reshape(shard_rows, heads_dev, HD).astype(jnp.float32), positions)
    rotated_q = rotated_q.astype(jnp.bfloat16).reshape(shard_rows, heads_dev * HD)
    rotated_k = rotate(
        keys_values[0, 0].reshape(shard_rows, kv_heads_dev, HD).astype(jnp.float32), positions
    )
    own_block = jnp.stack(
        [rotated_k.astype(jnp.bfloat16).reshape(shard_rows, width), keys_values[0, 1]]
    )
    outbox = jnp.broadcast_to(own_block[:, None], (2, seq_count, shard_rows, width))
    gathered = lax.all_to_all(
        outbox.reshape(2, seq_count * shard_rows, width), "seq", 1, 1, tiled=True
    )
    tokens = gathered.shape[1]

    reach_count = min(WINDOW // shard_rows, seq_count - 1)
    span = (reach_count + 1) * shard_rows
    key_start = jnp.maximum(first_pos - reach_count * shard_rows, 0)
    scalars = jnp.stack([seq_len, first_pos, key_start]).astype(jnp.int32)
    attended = attention(scalars, rotated_q, gathered, kv_heads_dev, group_size, span)
    attended = attended.reshape(1, shard_rows, heads_dev * HD)

    slot_rows = WINDOW // seq_count
    padded = jnp.concatenate([jnp.zeros((2, WINDOW, width), jnp.bfloat16), gathered], axis=1)
    begin_row = seq_len + seq_index * slot_rows
    window_cache = lax.dynamic_slice_in_dim(padded, begin_row, slot_rows, 1)
    del tokens
    return (attended, window_cache[None])


def solution(mesh):
    return jax.shard_map(
        local,
        mesh=mesh,
        in_specs=(
            P("section", ("parts", "seq"), "tp"),
            P("section", None, ("parts", "seq"), "tp"),
            P("parts"),
        ),
        out_specs=(
            P("section", ("parts", "seq"), "tp"),
            P("section", None, ("parts", "seq"), "tp"),
        ),
        check_vma=False,
    )
```

```python
import functools
import math

import jax
import jax.numpy as jnp
from jax import lax
from jax.experimental import pallas as pl
from jax.experimental.pallas import tpu as pltpu
from jax.sharding import PartitionSpec as P

HD = 128
WINDOW = 2048


rope_base = 1000000.0
neg_floor = -1e30


def rotate(field, positions):
    half_dim = field.shape[-1] // 2
    frequency = jnp.exp(
        jnp.arange(half_dim, dtype=jnp.float32) * (-2.0 * math.log(rope_base) / field.shape[-1])
    )
    angles = positions.astype(jnp.float32)[:, None] * frequency[None, :]
    cosine = jnp.cos(angles)[:, None, :]
    sine_part = jnp.sin(angles)[:, None, :]
    lower_half = field[..., :half_dim]
    upper_half = field[..., half_dim:]
    return jnp.concatenate(
        [
            lower_half * cosine - upper_half * sine_part,
            upper_half * cosine + lower_half * sine_part,
        ],
        axis=-1,
    )


def attend_kernel(scalars, q_ref, *refs, nblk, rows, group, init, final):
    kv_refs = refs[:nblk]
    refs = refs[nblk:]
    if not init:
        m_in, l_in, acc_in = refs[:3]
        refs = refs[3:]
    if final:
        o_ref, bias_ref = refs
    else:
        m_out, l_out, acc_out, bias_ref = refs
    seq_len = scalars[0]
    first_pos = scalars[1]
    key_first = scalars[2]
    blk = kv_refs[0].shape[1]
    span = nblk * blk
    query_pos = first_pos + lax.broadcasted_iota(jnp.int32, (rows, span), 0)
    key_pos = key_first + lax.broadcasted_iota(jnp.int32, (rows, span), 1)
    allowed = (
        (key_pos <= query_pos)
        & (key_pos > query_pos - WINDOW)
        & (key_pos >= 0)
        & (key_pos < seq_len)
    )
    bias_ref[...] = jnp.where(allowed, 0.0, neg_floor)
    valid = (first_pos + lax.broadcasted_iota(jnp.int32, (rows, 1), 0)) < seq_len
    scale = 1.0 / math.sqrt(HD)
    for head in range(group):
        cols = slice(head * HD, (head + 1) * HD)
        q = q_ref[:, cols]
        raws = [
            lax.dot_general(
                q, kv_refs[b][0], (((1,), (1,)), ((), ())), preferred_element_type=jnp.float32
            )
            + bias_ref[:, b * blk:(b + 1) * blk]
            for b in range(nblk)
        ]
        top = functools.reduce(
            jnp.maximum, [jnp.max(r, axis=-1, keepdims=True) for r in raws]
        )
        if not init:
            top_old = m_in[0, :, head:head + 1]
            top = jnp.maximum(top, top_old)
        weights = [jnp.exp((r - top) * scale) for r in raws]
        totals = functools.reduce(
            jnp.add, [jnp.sum(w, axis=-1, keepdims=True) for w in weights]
        )
        numer = functools.reduce(
            jnp.add,
            [
                jnp.dot(w.astype(jnp.bfloat16), kv_refs[b][1], preferred_element_type=jnp.float32)
                for b, w in enumerate(weights)
            ],
        )
        if not init:
            rescale = jnp.exp((top_old - top) * scale)
            totals = l_in[0, :, head:head + 1] * rescale + totals
            numer = acc_in[:, cols] * rescale + numer
        if final:
            denom = jnp.where(valid, totals, 1.0)
            o_ref[:, cols] = jnp.where(valid, numer / denom, 0.0).astype(o_ref.dtype)
        else:
            m_out[0, :, head:head + 1] = top
            l_out[0, :, head:head + 1] = totals
            acc_out[:, cols] = numer


def attend(scalars, rotated_q, blocks, state, kv_heads_dev, group_size, final):
    rows = rotated_q.shape[0]
    nblk = len(blocks)
    blk = blocks[0].shape[1]
    width = group_size * HD
    init = state is None
    kernel = functools.partial(
        attend_kernel, nblk=nblk, rows=rows, group=group_size, init=init, final=final
    )
    acc_spec = pl.BlockSpec((rows, width), lambda j, s: (0, j))
    top_spec = pl.BlockSpec((1, rows, group_size), lambda j, s: (j, 0, 0))
    in_specs = [acc_spec] + [pl.BlockSpec((2, blk, HD), lambda j, s: (0, 0, j))] * nblk
    operands = [rotated_q] + list(blocks)
    if not init:
        in_specs += [top_spec, top_spec, acc_spec]
        operands += list(state)
    top_shape = jax.ShapeDtypeStruct((kv_heads_dev, rows, group_size), jnp.float32)
    if final:
        out_specs = acc_spec
        out_shape = jax.ShapeDtypeStruct((rows, kv_heads_dev * width), jnp.bfloat16)
    else:
        out_specs = [top_spec, top_spec, acc_spec]
        out_shape = [
            top_shape,
            top_shape,
            jax.ShapeDtypeStruct((rows, kv_heads_dev * width), jnp.float32),
        ]
    grid_spec = pltpu.PrefetchScalarGridSpec(
        num_scalar_prefetch=1,
        grid=(kv_heads_dev,),
        in_specs=in_specs,
        out_specs=out_specs,
        scratch_shapes=[pltpu.VMEM((rows, nblk * blk), jnp.float32)],
    )
    return pl.pallas_call(kernel, grid_spec=grid_spec, out_shape=out_shape)(
        scalars, *operands
    )


def passed_along(x, by):
    devices = lax.axis_size("seq")
    pairs = [(i, i + by) for i in range(devices) if 0 <= i + by < devices]
    return lax.ppermute(x, "seq", pairs)


def local(queries, keys_values, lengths):
    seq_len = lengths[0]
    shard_rows = queries.shape[1]
    width = keys_values.shape[-1]
    kv_heads_dev = width // HD
    heads_dev = queries.shape[-1] // HD
    group_size = heads_dev // kv_heads_dev
    seq_index = lax.axis_index("seq")
    seq_count = lax.axis_size("seq")
    tokens = seq_count * shard_rows
    first_pos = seq_index * shard_rows
    positions = first_pos + jnp.arange(shard_rows, dtype=jnp.int32)
    rotated_k = rotate(
        keys_values[0, 0].reshape(shard_rows, kv_heads_dev, HD).astype(jnp.float32), positions
    )
    own_block = jnp.stack(
        [rotated_k.astype(jnp.bfloat16).reshape(shard_rows, width), keys_values[0, 1]]
    )
    reach_count = min(WINDOW // shard_rows, seq_count - 1)
    slot_rows = WINDOW // seq_count
    if WINDOW >= tokens:
        older = []
        moving = own_block
        for hop in range(reach_count):
            moving = passed_along(moving, 1)
            older.append(moving)
        shortest = min(WINDOW, tokens - shard_rows) + 1
        cache_hops = 0
        for index in range(seq_count):
            if tokens - WINDOW + (index + 1) * slot_rows - 1 < 0:
                continue
            lowest = max(0, (shortest - WINDOW + index * slot_rows) // shard_rows)
            cache_hops = max(cache_hops, index - lowest)
        cache_hops = min(cache_hops, reach_count)
        tail = jnp.concatenate(older[:cache_hops][::-1] + [own_block], axis=1)
        tail_first = first_pos - cache_hops * shard_rows
    else:
        outbox = jnp.broadcast_to(own_block[:, None], (2, seq_count, shard_rows, width))
        tail = lax.all_to_all(
            outbox.reshape(2, tokens, width), "seq", 1, 1, tiled=True
        )
        tail_first = 0
        older = [
            lax.dynamic_slice_in_dim(
                tail, jnp.maximum(seq_index - hop - 1, 0) * shard_rows, shard_rows, 1
            )
            for hop in range(reach_count)
        ]
    rotated_q = rotate(queries[0].reshape(shard_rows, heads_dev, HD).astype(jnp.float32), positions)
    rotated_q = rotated_q.astype(jnp.bfloat16).reshape(shard_rows, heads_dev * HD)

    def scalars_for(first_key):
        return jnp.stack([seq_len, first_pos, first_key]).astype(jnp.int32)

    stages = [[own_block]]
    if reach_count >= 2:
        stages.append(older[:reach_count - 1][::-1])
    if reach_count >= 1:
        stages.append([older[-1]])
    state = None
    for number, stage in enumerate(stages):
        final = number == len(stages) - 1
        first_key = first_pos - shard_rows * (
            0 if number == 0 else (reach_count - 1 if not final else reach_count)
        )
        state = attend(
            scalars_for(first_key), rotated_q, stage, state, kv_heads_dev, group_size, final
        )
    attended = state.reshape(1, shard_rows, heads_dev * HD)

    padded = jnp.concatenate([jnp.zeros((2, WINDOW, width), jnp.bfloat16), tail], axis=1)
    begin_row = seq_len - tail_first + seq_index * slot_rows
    window_cache = lax.dynamic_slice_in_dim(padded, begin_row, slot_rows, 1)
    return (attended, window_cache[None])


def solution(mesh):
    return jax.shard_map(
        local,
        mesh=mesh,
        in_specs=(
            P("section", ("parts", "seq"), "tp"),
            P("section", None, ("parts", "seq"), "tp"),
            P("parts"),
        ),
        out_specs=(
            P("section", ("parts", "seq"), "tp"),
            P("section", None, ("parts", "seq"), "tp"),
        ),
        check_vma=False,
    )
```

```python
import functools
import math

import jax
import jax.numpy as jnp
from jax import lax
from jax.experimental import pallas as pl
from jax.experimental.pallas import tpu as pltpu
from jax.sharding import PartitionSpec as P

HD = 128
WINDOW = 2048


rope_base = 1000000.0
neg_floor = -1e30


def rotate(field, positions):
    half_dim = field.shape[-1] // 2
    frequency = jnp.exp(
        jnp.arange(half_dim, dtype=jnp.float32) * (-2.0 * math.log(rope_base) / field.shape[-1])
    )
    angles = positions.astype(jnp.float32)[:, None] * frequency[None, :]
    cosine = jnp.cos(angles)[:, None, :]
    sine_part = jnp.sin(angles)[:, None, :]
    lower_half = field[..., :half_dim]
    upper_half = field[..., half_dim:]
    return jnp.concatenate(
        [
            lower_half * cosine - upper_half * sine_part,
            upper_half * cosine + lower_half * sine_part,
        ],
        axis=-1,
    )


def attend_kernel(scalars, q_ref, k_ref, v_ref, o_ref, bias_ref, *, rows, span, group):
    seq_len = scalars[0]
    first_pos = scalars[1]
    key_start = pl.multiple_of(scalars[2], 256)
    query_pos = first_pos + lax.broadcasted_iota(jnp.int32, (rows, span), 0)
    key_pos = scalars[3] + lax.broadcasted_iota(jnp.int32, (rows, span), 1)
    allowed = (
        (key_pos <= query_pos)
        & (key_pos > query_pos - WINDOW)
        & (key_pos >= 0)
        & (key_pos < seq_len)
    )
    bias_ref[...] = jnp.where(allowed, 0.0, neg_floor)
    k = k_ref[0, pl.ds(key_start, span), :]
    v = v_ref[0, pl.ds(key_start, span), :]
    valid = (first_pos + lax.broadcasted_iota(jnp.int32, (rows, 1), 0)) < seq_len
    scale = 1.0 / math.sqrt(HD)
    for head in range(group):
        cols = slice(head * HD, (head + 1) * HD)
        raw = lax.dot_general(
            q_ref[:, cols], k, (((1,), (1,)), ((), ())), preferred_element_type=jnp.float32
        ) + bias_ref[...]
        row_top = jnp.max(raw, axis=-1, keepdims=True)
        weights = jnp.exp((raw - row_top) * scale)
        totals = jnp.sum(weights, axis=-1, keepdims=True)
        numer = jnp.dot(weights.astype(jnp.bfloat16), v, preferred_element_type=jnp.float32)
        denom = jnp.where(valid, totals, 1.0)
        o_ref[:, cols] = jnp.where(valid, numer / denom, 0.0).astype(o_ref.dtype)


def attention(scalars, rotated_q, gathered, kv_heads_dev, group_size, span):
    rows = rotated_q.shape[0]
    tokens = gathered.shape[1]
    kernel = functools.partial(attend_kernel, rows=rows, span=span, group=group_size)
    width = group_size * HD
    grid_spec = pltpu.PrefetchScalarGridSpec(
        num_scalar_prefetch=1,
        grid=(kv_heads_dev,),
        in_specs=[
            pl.BlockSpec((rows, width), lambda j, s: (0, j)),
            pl.BlockSpec((1, tokens, HD), lambda j, s: (0, 0, j)),
            pl.BlockSpec((1, tokens, HD), lambda j, s: (1, 0, j)),
        ],
        out_specs=pl.BlockSpec((rows, width), lambda j, s: (0, j)),
        scratch_shapes=[pltpu.VMEM((rows, span), jnp.float32)],
    )
    return pl.pallas_call(
        kernel,
        grid_spec=grid_spec,
        out_shape=jax.ShapeDtypeStruct((rows, kv_heads_dev * width), jnp.bfloat16),
    )(scalars, rotated_q, gathered, gathered)


def passed_along(x, by):
    devices = lax.axis_size("seq")
    pairs = [(i, i + by) for i in range(devices) if 0 <= i + by < devices]
    return lax.ppermute(x, "seq", pairs)


def local(queries, keys_values, lengths):
    seq_len = lengths[0]
    shard_rows = queries.shape[1]
    width = keys_values.shape[-1]
    kv_heads_dev = width // HD
    heads_dev = queries.shape[-1] // HD
    group_size = heads_dev // kv_heads_dev
    seq_index = lax.axis_index("seq")
    seq_count = lax.axis_size("seq")
    tokens = seq_count * shard_rows
    first_pos = seq_index * shard_rows
    positions = first_pos + jnp.arange(shard_rows, dtype=jnp.int32)
    rotated_q = rotate(queries[0].reshape(shard_rows, heads_dev, HD).astype(jnp.float32), positions)
    rotated_q = rotated_q.astype(jnp.bfloat16).reshape(shard_rows, heads_dev * HD)
    rotated_k = rotate(
        keys_values[0, 0].reshape(shard_rows, kv_heads_dev, HD).astype(jnp.float32), positions
    )
    own_block = jnp.stack(
        [rotated_k.astype(jnp.bfloat16).reshape(shard_rows, width), keys_values[0, 1]]
    )
    reach_count = min(WINDOW // shard_rows, seq_count - 1)
    span = (reach_count + 1) * shard_rows
    if WINDOW >= tokens:
        shifted = [own_block]
        for hop in range(1, reach_count + 1):
            shifted.insert(0, passed_along(own_block, hop))
        held = jnp.concatenate(shifted, axis=1)
        held_first = first_pos - reach_count * shard_rows
        key_index = jnp.zeros((), jnp.int32)
        key_first = held_first
    else:
        outbox = jnp.broadcast_to(own_block[:, None], (2, seq_count, shard_rows, width))
        held = lax.all_to_all(
            outbox.reshape(2, tokens, width), "seq", 1, 1, tiled=True
        )
        held_first = 0
        key_index = jnp.maximum(first_pos - reach_count * shard_rows, 0)
        key_first = key_index
    scalars = jnp.stack([seq_len, first_pos, key_index, key_first]).astype(jnp.int32)
    attended = attention(scalars, rotated_q, held, kv_heads_dev, group_size, span)
    attended = attended.reshape(1, shard_rows, heads_dev * HD)

    slot_rows = WINDOW // seq_count
    padded = jnp.concatenate([jnp.zeros((2, WINDOW, width), jnp.bfloat16), held], axis=1)
    begin_row = seq_len - held_first + seq_index * slot_rows
    window_cache = lax.dynamic_slice_in_dim(padded, begin_row, slot_rows, 1)
    return (attended, window_cache[None])


def solution(mesh):
    return jax.shard_map(
        local,
        mesh=mesh,
        in_specs=(
            P("section", ("parts", "seq"), "tp"),
            P("section", None, ("parts", "seq"), "tp"),
            P("parts"),
        ),
        out_specs=(
            P("section", ("parts", "seq"), "tp"),
            P("section", None, ("parts", "seq"), "tp"),
        ),
        check_vma=False,
    )
```

```python
import functools
import math

import jax
import jax.numpy as jnp
from jax import lax
from jax.experimental import pallas as pl
from jax.experimental.pallas import tpu as pltpu
from jax.sharding import PartitionSpec as P

HD = 128
WINDOW = 2048


rope_base = 1000000.0
neg_floor = -1e30


def rotate(field, positions):
    half_dim = field.shape[-1] // 2
    frequency = jnp.exp(
        jnp.arange(half_dim, dtype=jnp.float32) * (-2.0 * math.log(rope_base) / field.shape[-1])
    )
    angles = positions.astype(jnp.float32)[:, None] * frequency[None, :]
    cosine = jnp.cos(angles)[:, None, :]
    sine_part = jnp.sin(angles)[:, None, :]
    lower_half = field[..., :half_dim]
    upper_half = field[..., half_dim:]
    return jnp.concatenate(
        [
            lower_half * cosine - upper_half * sine_part,
            upper_half * cosine + lower_half * sine_part,
        ],
        axis=-1,
    )


def attend_kernel(scalars, q_ref, *refs, rows, span, group, nparts):
    part_refs = refs[:nparts]
    o_ref, bias_ref = refs[nparts:]
    seq_len = scalars[0]
    first_pos = scalars[1]
    key_start = pl.multiple_of(scalars[2], 256)
    query_pos = first_pos + lax.broadcasted_iota(jnp.int32, (rows, span), 0)
    key_pos = scalars[3] + lax.broadcasted_iota(jnp.int32, (rows, span), 1)
    allowed = (
        (key_pos <= query_pos)
        & (key_pos > query_pos - WINDOW)
        & (key_pos >= 0)
        & (key_pos < seq_len)
    )
    bias_ref[...] = jnp.where(allowed, 0.0, neg_floor)
    if nparts == 1:
        k = part_refs[0][0, pl.ds(key_start, span), :]
        v = part_refs[0][1, pl.ds(key_start, span), :]
    else:
        k = jnp.concatenate([p[0] for p in part_refs], axis=0)
        v = jnp.concatenate([p[1] for p in part_refs], axis=0)
    valid = (first_pos + lax.broadcasted_iota(jnp.int32, (rows, 1), 0)) < seq_len
    scale = 1.0 / math.sqrt(HD)
    for head in range(group):
        cols = slice(head * HD, (head + 1) * HD)
        raw = lax.dot_general(
            q_ref[:, cols], k, (((1,), (1,)), ((), ())), preferred_element_type=jnp.float32
        ) + bias_ref[...]
        row_top = jnp.max(raw, axis=-1, keepdims=True)
        weights = jnp.exp((raw - row_top) * scale)
        totals = jnp.sum(weights, axis=-1, keepdims=True)
        numer = jnp.dot(weights.astype(jnp.bfloat16), v, preferred_element_type=jnp.float32)
        denom = jnp.where(valid, totals, 1.0)
        o_ref[:, cols] = jnp.where(valid, numer / denom, 0.0).astype(o_ref.dtype)


def attention(scalars, rotated_q, parts, kv_heads_dev, group_size, span):
    rows = rotated_q.shape[0]
    nparts = len(parts)
    kernel = functools.partial(
        attend_kernel, rows=rows, span=span, group=group_size, nparts=nparts
    )
    width = group_size * HD
    grid_spec = pltpu.PrefetchScalarGridSpec(
        num_scalar_prefetch=1,
        grid=(kv_heads_dev,),
        in_specs=[pl.BlockSpec((rows, width), lambda j, s: (0, j))]
        + [pl.BlockSpec((2, p.shape[1], HD), lambda j, s: (0, 0, j)) for p in parts],
        out_specs=pl.BlockSpec((rows, width), lambda j, s: (0, j)),
        scratch_shapes=[pltpu.VMEM((rows, span), jnp.float32)],
    )
    return pl.pallas_call(
        kernel,
        grid_spec=grid_spec,
        out_shape=jax.ShapeDtypeStruct((rows, kv_heads_dev * width), jnp.bfloat16),
    )(scalars, rotated_q, *parts)


def passed_along(x, by):
    devices = lax.axis_size("seq")
    pairs = [(i, i + by) for i in range(devices) if 0 <= i + by < devices]
    return lax.ppermute(x, "seq", pairs)


def local(queries, keys_values, lengths):
    seq_len = lengths[0]
    shard_rows = queries.shape[1]
    width = keys_values.shape[-1]
    kv_heads_dev = width // HD
    heads_dev = queries.shape[-1] // HD
    group_size = heads_dev // kv_heads_dev
    seq_index = lax.axis_index("seq")
    seq_count = lax.axis_size("seq")
    tokens = seq_count * shard_rows
    first_pos = seq_index * shard_rows
    positions = first_pos + jnp.arange(shard_rows, dtype=jnp.int32)
    rotated_q = rotate(queries[0].reshape(shard_rows, heads_dev, HD).astype(jnp.float32), positions)
    rotated_q = rotated_q.astype(jnp.bfloat16).reshape(shard_rows, heads_dev * HD)
    rotated_k = rotate(
        keys_values[0, 0].reshape(shard_rows, kv_heads_dev, HD).astype(jnp.float32), positions
    )
    own_block = jnp.stack(
        [rotated_k.astype(jnp.bfloat16).reshape(shard_rows, width), keys_values[0, 1]]
    )
    reach_count = min(WINDOW // shard_rows, seq_count - 1)
    span = (reach_count + 1) * shard_rows
    slot_rows = WINDOW // seq_count
    if WINDOW >= tokens:
        shifted = [own_block]
        for hop in range(1, reach_count + 1):
            shifted.insert(0, passed_along(own_block, hop))
        parts = shifted
        key_index = jnp.zeros((), jnp.int32)
        key_first = first_pos - reach_count * shard_rows
        shortest = min(WINDOW, tokens - shard_rows) + 1
        cache_hops = 0
        for index in range(seq_count):
            if tokens - WINDOW + (index + 1) * slot_rows - 1 < 0:
                continue
            lowest = max(0, (shortest - WINDOW + index * slot_rows) // shard_rows)
            cache_hops = max(cache_hops, index - lowest)
        cache_hops = min(cache_hops, reach_count)
        held = jnp.concatenate(shifted[reach_count - cache_hops:], axis=1)
        held_first = first_pos - cache_hops * shard_rows
    else:
        outbox = jnp.broadcast_to(own_block[:, None], (2, seq_count, shard_rows, width))
        held = lax.all_to_all(
            outbox.reshape(2, tokens, width), "seq", 1, 1, tiled=True
        )
        parts = [held]
        held_first = 0
        key_index = jnp.maximum(first_pos - reach_count * shard_rows, 0)
        key_first = key_index
    scalars = jnp.stack([seq_len, first_pos, key_index, key_first]).astype(jnp.int32)
    attended = attention(scalars, rotated_q, parts, kv_heads_dev, group_size, span)
    attended = attended.reshape(1, shard_rows, heads_dev * HD)

    padded = jnp.concatenate([jnp.zeros((2, WINDOW, width), jnp.bfloat16), held], axis=1)
    begin_row = seq_len - held_first + seq_index * slot_rows
    window_cache = lax.dynamic_slice_in_dim(padded, begin_row, slot_rows, 1)
    return (attended, window_cache[None])


def solution(mesh):
    return jax.shard_map(
        local,
        mesh=mesh,
        in_specs=(
            P("section", ("parts", "seq"), "tp"),
            P("section", None, ("parts", "seq"), "tp"),
            P("parts"),
        ),
        out_specs=(
            P("section", ("parts", "seq"), "tp"),
            P("section", None, ("parts", "seq"), "tp"),
        ),
        check_vma=False,
    )
```

```python
import functools
import math

import jax
import jax.numpy as jnp
from jax import lax
from jax.experimental import pallas as pl
from jax.experimental.pallas import tpu as pltpu
from jax.sharding import PartitionSpec as P

HD = 128
WINDOW = 2048


rope_base = 1000000.0
neg_floor = -1e30


def rotate(field, positions):
    half_dim = field.shape[-1] // 2
    frequency = jnp.exp(
        jnp.arange(half_dim, dtype=jnp.float32) * (-2.0 * math.log(rope_base) / field.shape[-1])
    )
    angles = positions.astype(jnp.float32)[:, None] * frequency[None, :]
    cosine = jnp.cos(angles)[:, None, :]
    sine_part = jnp.sin(angles)[:, None, :]
    lower_half = field[..., :half_dim]
    upper_half = field[..., half_dim:]
    return jnp.concatenate(
        [
            lower_half * cosine - upper_half * sine_part,
            upper_half * cosine + lower_half * sine_part,
        ],
        axis=-1,
    )


def attend_kernel(scalars, q_ref, *refs, rows, span, group, nparts):
    part_refs = refs[:nparts]
    o_ref, bias_ref = refs[nparts:]
    seq_len = scalars[0]
    first_pos = scalars[1]
    key_start = pl.multiple_of(scalars[2], 256)
    query_pos = first_pos + lax.broadcasted_iota(jnp.int32, (rows, span), 0)
    key_pos = scalars[3] + lax.broadcasted_iota(jnp.int32, (rows, span), 1)
    allowed = (
        (key_pos <= query_pos)
        & (key_pos > query_pos - WINDOW)
        & (key_pos >= 0)
        & (key_pos < seq_len)
    )
    bias_ref[...] = jnp.where(allowed, 0.0, neg_floor)
    if nparts == 1:
        k = part_refs[0][0, pl.ds(key_start, span), :]
        v = part_refs[0][1, pl.ds(key_start, span), :]
    else:
        k = jnp.concatenate([p[0] for p in part_refs], axis=0)
        v = jnp.concatenate([p[1] for p in part_refs], axis=0)
    valid = (first_pos + lax.broadcasted_iota(jnp.int32, (rows, 1), 0)) < seq_len
    scale = 1.0 / math.sqrt(HD)
    for head in range(group):
        cols = slice(head * HD, (head + 1) * HD)
        raw = lax.dot_general(
            q_ref[:, cols], k, (((1,), (1,)), ((), ())), preferred_element_type=jnp.float32
        ) + bias_ref[...]
        row_top = jnp.max(raw, axis=-1, keepdims=True)
        weights = jnp.exp((raw - row_top) * scale)
        totals = jnp.sum(weights, axis=-1, keepdims=True)
        numer = jnp.dot(weights.astype(jnp.bfloat16), v, preferred_element_type=jnp.float32)
        denom = jnp.where(valid, totals, 1.0)
        o_ref[:, cols] = jnp.where(valid, numer / denom, 0.0).astype(o_ref.dtype)


def attention(scalars, rotated_q, parts, kv_heads_dev, group_size, span):
    rows = rotated_q.shape[0]
    nparts = len(parts)
    kernel = functools.partial(
        attend_kernel, rows=rows, span=span, group=group_size, nparts=nparts
    )
    width = group_size * HD
    grid_spec = pltpu.PrefetchScalarGridSpec(
        num_scalar_prefetch=1,
        grid=(kv_heads_dev,),
        in_specs=[pl.BlockSpec((rows, width), lambda j, s: (0, j))]
        + [pl.BlockSpec((2, p.shape[1], HD), lambda j, s: (0, 0, j)) for p in parts],
        out_specs=pl.BlockSpec((rows, width), lambda j, s: (0, j)),
        scratch_shapes=[pltpu.VMEM((rows, span), jnp.float32)],
    )
    return pl.pallas_call(
        kernel,
        grid_spec=grid_spec,
        out_shape=jax.ShapeDtypeStruct((rows, kv_heads_dev * width), jnp.bfloat16),
    )(scalars, rotated_q, *parts)


def passed_along(x, by):
    devices = lax.axis_size("seq")
    pairs = [(i, i + by) for i in range(devices) if 0 <= i + by < devices]
    return lax.ppermute(x, "seq", pairs)


def local(queries, keys_values, lengths):
    seq_len = lengths[0]
    shard_rows = queries.shape[1]
    width = keys_values.shape[-1]
    kv_heads_dev = width // HD
    heads_dev = queries.shape[-1] // HD
    group_size = heads_dev // kv_heads_dev
    seq_index = lax.axis_index("seq")
    seq_count = lax.axis_size("seq")
    tokens = seq_count * shard_rows
    first_pos = seq_index * shard_rows
    positions = first_pos + jnp.arange(shard_rows, dtype=jnp.int32)
    rotated_q = rotate(queries[0].reshape(shard_rows, heads_dev, HD).astype(jnp.float32), positions)
    rotated_q = rotated_q.astype(jnp.bfloat16).reshape(shard_rows, heads_dev * HD)
    rotated_k = rotate(
        keys_values[0, 0].reshape(shard_rows, kv_heads_dev, HD).astype(jnp.float32), positions
    )
    own_block = jnp.stack(
        [rotated_k.astype(jnp.bfloat16).reshape(shard_rows, width), keys_values[0, 1]]
    )
    reach_count = min(WINDOW // shard_rows, seq_count - 1)
    span = (reach_count + 1) * shard_rows
    slot_rows = WINDOW // seq_count
    if WINDOW >= tokens:
        shifted = [own_block]
        for hop in range(1, reach_count + 1):
            shifted.insert(0, passed_along(own_block, hop))
        parts = shifted
        key_index = jnp.zeros((), jnp.int32)
        key_first = first_pos - reach_count * shard_rows
        shortest = min(WINDOW, tokens - shard_rows) + 1
        cache_hops = 0
        for index in range(seq_count):
            if tokens - WINDOW + (index + 1) * slot_rows - 1 < 0:
                continue
            lowest = max(0, (shortest - WINDOW + index * slot_rows) // shard_rows)
            cache_hops = max(cache_hops, index - lowest)
        cache_hops = min(cache_hops, reach_count)
        held = jnp.concatenate(shifted[reach_count - cache_hops:], axis=1)
        held_first = first_pos - cache_hops * shard_rows
    else:
        outbox = jnp.broadcast_to(own_block[:, None], (2, seq_count, shard_rows, width))
        held = lax.all_to_all(
            outbox.reshape(2, tokens, width), "seq", 1, 1, tiled=True
        )
        parts = [held]
        held_first = 0
        key_index = jnp.maximum(first_pos - reach_count * shard_rows, 0)
        key_first = key_index
    scalars = jnp.stack([seq_len, first_pos, key_index, key_first]).astype(jnp.int32)
    attended = attention(scalars, rotated_q, parts, kv_heads_dev, group_size, span)
    attended = attended.reshape(1, shard_rows, heads_dev * HD)

    padded = jnp.concatenate([jnp.zeros((2, slot_rows, width), jnp.bfloat16), held], axis=1)
    begin_row = seq_len - WINDOW - held_first + seq_index * slot_rows + slot_rows
    window_cache = lax.dynamic_slice_in_dim(padded, jnp.maximum(begin_row, 0), slot_rows, 1)
    return (attended, window_cache[None])


def solution(mesh):
    return jax.shard_map(
        local,
        mesh=mesh,
        in_specs=(
            P("section", ("parts", "seq"), "tp"),
            P("section", None, ("parts", "seq"), "tp"),
            P("parts"),
        ),
        out_specs=(
            P("section", ("parts", "seq"), "tp"),
            P("section", None, ("parts", "seq"), "tp"),
        ),
        check_vma=False,
    )
```

```python
import functools
import math

import jax
import jax.numpy as jnp
from jax import lax
from jax.experimental import pallas as pl
from jax.experimental.pallas import tpu as pltpu
from jax.sharding import PartitionSpec as P

HD = 128
WINDOW = 2048


rope_base = 1000000.0
neg_floor = -1e30


def rotate(field, positions):
    half_dim = field.shape[-1] // 2
    frequency = jnp.exp(
        jnp.arange(half_dim, dtype=jnp.float32) * (-2.0 * math.log(rope_base) / field.shape[-1])
    )
    angles = positions.astype(jnp.float32)[:, None] * frequency[None, :]
    cosine = jnp.cos(angles)[:, None, :]
    sine_part = jnp.sin(angles)[:, None, :]
    lower_half = field[..., :half_dim]
    upper_half = field[..., half_dim:]
    return jnp.concatenate(
        [
            lower_half * cosine - upper_half * sine_part,
            upper_half * cosine + lower_half * sine_part,
        ],
        axis=-1,
    )


def rotate_flat(field, positions):
    rows, width = field.shape
    half_dim = HD // 2
    frequency = jnp.exp(
        jnp.arange(half_dim, dtype=jnp.float32) * (-2.0 * math.log(rope_base) / HD)
    )
    angles = positions.astype(jnp.float32)[:, None] * frequency[None, :]
    cosine = jnp.cos(angles)
    sine_part = jnp.sin(angles)
    heads = width // HD
    cos_full = jnp.tile(jnp.concatenate([cosine, cosine], axis=1), (1, heads))
    sin_signed = jnp.tile(jnp.concatenate([-sine_part, sine_part], axis=1), (1, heads))
    wide = field.astype(jnp.float32)
    swapped = jnp.roll(wide.reshape(rows, heads, HD), half_dim, axis=-1).reshape(rows, width)
    return wide * cos_full + swapped * sin_signed


def attend_kernel(scalars, q_ref, *refs, rows, span, group, nparts):
    part_refs = refs[:nparts]
    o_ref, bias_ref = refs[nparts:]
    seq_len = scalars[0]
    first_pos = scalars[1]
    key_start = pl.multiple_of(scalars[2], 256)
    query_pos = first_pos + lax.broadcasted_iota(jnp.int32, (rows, span), 0)
    key_pos = scalars[3] + lax.broadcasted_iota(jnp.int32, (rows, span), 1)
    allowed = (
        (key_pos <= query_pos)
        & (key_pos > query_pos - WINDOW)
        & (key_pos >= 0)
        & (key_pos < seq_len)
    )
    bias_ref[...] = jnp.where(allowed, 0.0, neg_floor)
    if nparts == 1:
        k = part_refs[0][0, pl.ds(key_start, span), :]
        v = part_refs[0][1, pl.ds(key_start, span), :]
    else:
        k = jnp.concatenate([p[0] for p in part_refs], axis=0)
        v = jnp.concatenate([p[1] for p in part_refs], axis=0)
    valid = (first_pos + lax.broadcasted_iota(jnp.int32, (rows, 1), 0)) < seq_len
    scale = 1.0 / math.sqrt(HD)
    for head in range(group):
        cols = slice(head * HD, (head + 1) * HD)
        raw = lax.dot_general(
            q_ref[:, cols], k, (((1,), (1,)), ((), ())), preferred_element_type=jnp.float32
        ) + bias_ref[...]
        row_top = jnp.max(raw, axis=-1, keepdims=True)
        weights = jnp.exp((raw - row_top) * scale)
        totals = jnp.sum(weights, axis=-1, keepdims=True)
        numer = jnp.dot(weights.astype(jnp.bfloat16), v, preferred_element_type=jnp.float32)
        denom = jnp.where(valid, totals, 1.0)
        o_ref[:, cols] = jnp.where(valid, numer / denom, 0.0).astype(o_ref.dtype)


def attention(scalars, rotated_q, parts, kv_heads_dev, group_size, span):
    rows = rotated_q.shape[0]
    nparts = len(parts)
    kernel = functools.partial(
        attend_kernel, rows=rows, span=span, group=group_size, nparts=nparts
    )
    width = group_size * HD
    grid_spec = pltpu.PrefetchScalarGridSpec(
        num_scalar_prefetch=1,
        grid=(kv_heads_dev,),
        in_specs=[pl.BlockSpec((rows, width), lambda j, s: (0, j))]
        + [pl.BlockSpec((2, p.shape[1], HD), lambda j, s: (0, 0, j)) for p in parts],
        out_specs=pl.BlockSpec((rows, width), lambda j, s: (0, j)),
        scratch_shapes=[pltpu.VMEM((rows, span), jnp.float32)],
    )
    return pl.pallas_call(
        kernel,
        grid_spec=grid_spec,
        out_shape=jax.ShapeDtypeStruct((rows, kv_heads_dev * width), jnp.bfloat16),
    )(scalars, rotated_q, *parts)


def passed_along(x, by):
    devices = lax.axis_size("seq")
    pairs = [(i, i + by) for i in range(devices) if 0 <= i + by < devices]
    return lax.ppermute(x, "seq", pairs)


def local(queries, keys_values, lengths):
    seq_len = lengths[0]
    shard_rows = queries.shape[1]
    width = keys_values.shape[-1]
    kv_heads_dev = width // HD
    heads_dev = queries.shape[-1] // HD
    group_size = heads_dev // kv_heads_dev
    seq_index = lax.axis_index("seq")
    seq_count = lax.axis_size("seq")
    tokens = seq_count * shard_rows
    first_pos = seq_index * shard_rows
    positions = first_pos + jnp.arange(shard_rows, dtype=jnp.int32)
    rotated_q = rotate(queries[0].reshape(shard_rows, heads_dev, HD).astype(jnp.float32), positions)
    rotated_q = rotated_q.astype(jnp.bfloat16).reshape(shard_rows, heads_dev * HD)
    rotated_k = rotate_flat(keys_values[0, 0], positions)
    own_block = jnp.stack([rotated_k.astype(jnp.bfloat16), keys_values[0, 1]])
    reach_count = min(WINDOW // shard_rows, seq_count - 1)
    span = (reach_count + 1) * shard_rows
    slot_rows = WINDOW // seq_count
    if WINDOW >= tokens:
        shifted = [own_block]
        for hop in range(1, reach_count + 1):
            shifted.insert(0, passed_along(own_block, hop))
        parts = shifted
        key_index = jnp.zeros((), jnp.int32)
        key_first = first_pos - reach_count * shard_rows
        shortest = min(WINDOW, tokens - shard_rows) + 1
        cache_hops = 0
        for index in range(seq_count):
            if tokens - WINDOW + (index + 1) * slot_rows - 1 < 0:
                continue
            lowest = max(0, (shortest - WINDOW + index * slot_rows) // shard_rows)
            cache_hops = max(cache_hops, index - lowest)
        cache_hops = min(cache_hops, reach_count)
        held = jnp.concatenate(shifted[reach_count - cache_hops:], axis=1)
        held_first = first_pos - cache_hops * shard_rows
    else:
        outbox = jnp.broadcast_to(own_block[:, None], (2, seq_count, shard_rows, width))
        held = lax.all_to_all(
            outbox.reshape(2, tokens, width), "seq", 1, 1, tiled=True
        )
        parts = [held]
        held_first = 0
        key_index = jnp.maximum(first_pos - reach_count * shard_rows, 0)
        key_first = key_index
    scalars = jnp.stack([seq_len, first_pos, key_index, key_first]).astype(jnp.int32)
    attended = attention(scalars, rotated_q, parts, kv_heads_dev, group_size, span)
    attended = attended.reshape(1, shard_rows, heads_dev * HD)

    padded = jnp.concatenate([jnp.zeros((2, slot_rows, width), jnp.bfloat16), held], axis=1)
    begin_row = seq_len - WINDOW - held_first + seq_index * slot_rows + slot_rows
    window_cache = lax.dynamic_slice_in_dim(padded, jnp.maximum(begin_row, 0), slot_rows, 1)
    return (attended, window_cache[None])


def solution(mesh):
    return jax.shard_map(
        local,
        mesh=mesh,
        in_specs=(
            P("section", ("parts", "seq"), "tp"),
            P("section", None, ("parts", "seq"), "tp"),
            P("parts"),
        ),
        out_specs=(
            P("section", ("parts", "seq"), "tp"),
            P("section", None, ("parts", "seq"), "tp"),
        ),
        check_vma=False,
    )
```

```python
import functools
import math

import jax
import jax.numpy as jnp
from jax import lax
from jax.experimental import pallas as pl
from jax.experimental.pallas import tpu as pltpu
from jax.sharding import PartitionSpec as P

HD = 128
WINDOW = 2048


rope_base = 1000000.0
neg_floor = -1e30


def rotate(field, positions):
    half_dim = field.shape[-1] // 2
    frequency = jnp.exp(
        jnp.arange(half_dim, dtype=jnp.float32) * (-2.0 * math.log(rope_base) / field.shape[-1])
    )
    angles = positions.astype(jnp.float32)[:, None] * frequency[None, :]
    cosine = jnp.cos(angles)[:, None, :]
    sine_part = jnp.sin(angles)[:, None, :]
    lower_half = field[..., :half_dim]
    upper_half = field[..., half_dim:]
    return jnp.concatenate(
        [
            lower_half * cosine - upper_half * sine_part,
            upper_half * cosine + lower_half * sine_part,
        ],
        axis=-1,
    )


def attend_kernel(scalars, q_ref, *refs, rows, span, group, nparts, slots):
    part_refs = refs[:nparts]
    if slots:
        o_ref, cache_ref, bias_ref = refs[nparts:]
    else:
        o_ref, bias_ref = refs[nparts:]
    seq_len = scalars[0]
    first_pos = scalars[1]
    key_start = pl.multiple_of(scalars[2], 256)
    query_pos = first_pos + lax.broadcasted_iota(jnp.int32, (rows, span), 0)
    key_pos = scalars[3] + lax.broadcasted_iota(jnp.int32, (rows, span), 1)
    allowed = (
        (key_pos <= query_pos)
        & (key_pos > query_pos - WINDOW)
        & (key_pos >= 0)
        & (key_pos < seq_len)
    )
    bias_ref[...] = jnp.where(allowed, 0.0, neg_floor)
    if nparts == 1:
        k = part_refs[0][0, pl.ds(key_start, span), :]
        v = part_refs[0][1, pl.ds(key_start, span), :]
    else:
        k = jnp.concatenate([p[0] for p in part_refs], axis=0)
        v = jnp.concatenate([p[1] for p in part_refs], axis=0)
    if slots:
        slot_pos = scalars[4] + lax.broadcasted_iota(jnp.int32, (slots, span), 0)
        held_pos = scalars[3] + lax.broadcasted_iota(jnp.int32, (slots, span), 1)
        pick = ((held_pos == slot_pos) & (slot_pos >= 0)).astype(jnp.bfloat16)
        cache_ref[0] = jnp.dot(pick, k, preferred_element_type=jnp.float32).astype(cache_ref.dtype)
        cache_ref[1] = jnp.dot(pick, v, preferred_element_type=jnp.float32).astype(cache_ref.dtype)
    valid = (first_pos + lax.broadcasted_iota(jnp.int32, (rows, 1), 0)) < seq_len
    scale = 1.0 / math.sqrt(HD)
    for head in range(group):
        cols = slice(head * HD, (head + 1) * HD)
        raw = lax.dot_general(
            q_ref[:, cols], k, (((1,), (1,)), ((), ())), preferred_element_type=jnp.float32
        ) + bias_ref[...]
        row_top = jnp.max(raw, axis=-1, keepdims=True)
        weights = jnp.exp((raw - row_top) * scale)
        totals = jnp.sum(weights, axis=-1, keepdims=True)
        numer = jnp.dot(weights.astype(jnp.bfloat16), v, preferred_element_type=jnp.float32)
        denom = jnp.where(valid, totals, 1.0)
        o_ref[:, cols] = jnp.where(valid, numer / denom, 0.0).astype(o_ref.dtype)


def attention(scalars, rotated_q, parts, kv_heads_dev, group_size, span, slots):
    rows = rotated_q.shape[0]
    nparts = len(parts)
    kernel = functools.partial(
        attend_kernel, rows=rows, span=span, group=group_size, nparts=nparts, slots=slots
    )
    width = group_size * HD
    out_specs = pl.BlockSpec((rows, width), lambda j, s: (0, j))
    out_shape = jax.ShapeDtypeStruct((rows, kv_heads_dev * width), jnp.bfloat16)
    if slots:
        out_specs = [out_specs, pl.BlockSpec((2, slots, HD), lambda j, s: (0, 0, j))]
        out_shape = [
            out_shape,
            jax.ShapeDtypeStruct((2, slots, kv_heads_dev * HD), jnp.bfloat16),
        ]
    grid_spec = pltpu.PrefetchScalarGridSpec(
        num_scalar_prefetch=1,
        grid=(kv_heads_dev,),
        in_specs=[pl.BlockSpec((rows, width), lambda j, s: (0, j))]
        + [pl.BlockSpec((2, p.shape[1], HD), lambda j, s: (0, 0, j)) for p in parts],
        out_specs=out_specs,
        scratch_shapes=[pltpu.VMEM((rows, span), jnp.float32)],
    )
    return pl.pallas_call(kernel, grid_spec=grid_spec, out_shape=out_shape)(
        scalars, rotated_q, *parts
    )


def passed_along(x, by):
    devices = lax.axis_size("seq")
    pairs = [(i, i + by) for i in range(devices) if 0 <= i + by < devices]
    return lax.ppermute(x, "seq", pairs)


def local(queries, keys_values, lengths):
    seq_len = lengths[0]
    shard_rows = queries.shape[1]
    width = keys_values.shape[-1]
    kv_heads_dev = width // HD
    heads_dev = queries.shape[-1] // HD
    group_size = heads_dev // kv_heads_dev
    seq_index = lax.axis_index("seq")
    seq_count = lax.axis_size("seq")
    tokens = seq_count * shard_rows
    first_pos = seq_index * shard_rows
    positions = first_pos + jnp.arange(shard_rows, dtype=jnp.int32)
    rotated_q = rotate(queries[0].reshape(shard_rows, heads_dev, HD).astype(jnp.float32), positions)
    rotated_q = rotated_q.astype(jnp.bfloat16).reshape(shard_rows, heads_dev * HD)
    rotated_k = rotate(
        keys_values[0, 0].reshape(shard_rows, kv_heads_dev, HD).astype(jnp.float32), positions
    )
    own_block = jnp.stack(
        [rotated_k.astype(jnp.bfloat16).reshape(shard_rows, width), keys_values[0, 1]]
    )
    reach_count = min(WINDOW // shard_rows, seq_count - 1)
    span = (reach_count + 1) * shard_rows
    slot_rows = WINDOW // seq_count
    if WINDOW >= tokens:
        shifted = [own_block]
        for hop in range(1, reach_count + 1):
            shifted.insert(0, passed_along(own_block, hop))
        parts = shifted
        key_index = jnp.zeros((), jnp.int32)
        key_first = first_pos - reach_count * shard_rows
    else:
        outbox = jnp.broadcast_to(own_block[:, None], (2, seq_count, shard_rows, width))
        held = lax.all_to_all(
            outbox.reshape(2, tokens, width), "seq", 1, 1, tiled=True
        )
        parts = [held]
        held_first = 0
        key_index = jnp.maximum(first_pos - reach_count * shard_rows, 0)
        key_first = key_index
    slot_first = seq_len - WINDOW + seq_index * slot_rows
    scalars = jnp.stack([seq_len, first_pos, key_index, key_first, slot_first]).astype(jnp.int32)
    if WINDOW >= tokens:
        attended, window_cache = attention(
            scalars, rotated_q, parts, kv_heads_dev, group_size, span, slot_rows
        )
    else:
        attended = attention(scalars, rotated_q, parts, kv_heads_dev, group_size, span, 0)
        padded = jnp.concatenate([jnp.zeros((2, slot_rows, width), jnp.bfloat16), held], axis=1)
        begin_row = slot_first - held_first + slot_rows
        window_cache = lax.dynamic_slice_in_dim(padded, jnp.maximum(begin_row, 0), slot_rows, 1)
    attended = attended.reshape(1, shard_rows, heads_dev * HD)
    return (attended, window_cache[None])


def solution(mesh):
    return jax.shard_map(
        local,
        mesh=mesh,
        in_specs=(
            P("section", ("parts", "seq"), "tp"),
            P("section", None, ("parts", "seq"), "tp"),
            P("parts"),
        ),
        out_specs=(
            P("section", ("parts", "seq"), "tp"),
            P("section", None, ("parts", "seq"), "tp"),
        ),
        check_vma=False,
    )
```

```python
import functools
import math

import jax
import jax.numpy as jnp
from jax import lax
from jax.experimental import pallas as pl
from jax.experimental.pallas import tpu as pltpu
from jax.sharding import PartitionSpec as P

HD = 128
WINDOW = 2048


rope_base = 1000000.0
neg_floor = -1e30


def rotate(field, positions):
    half_dim = field.shape[-1] // 2
    frequency = jnp.exp(
        jnp.arange(half_dim, dtype=jnp.float32) * (-2.0 * math.log(rope_base) / field.shape[-1])
    )
    angles = positions.astype(jnp.float32)[:, None] * frequency[None, :]
    cosine = jnp.cos(angles)[:, None, :]
    sine_part = jnp.sin(angles)[:, None, :]
    lower_half = field[..., :half_dim]
    upper_half = field[..., half_dim:]
    return jnp.concatenate(
        [
            lower_half * cosine - upper_half * sine_part,
            upper_half * cosine + lower_half * sine_part,
        ],
        axis=-1,
    )


def attend_kernel(scalars, q_ref, *refs, rows, span, group, nparts, slots):
    part_refs = refs[:nparts]
    if slots:
        o_ref, cache_ref, bias_ref = refs[nparts:]
    else:
        o_ref, bias_ref = refs[nparts:]
    seq_len = scalars[0]
    first_pos = scalars[1]
    key_start = pl.multiple_of(scalars[2], 256)
    query_pos = first_pos + lax.broadcasted_iota(jnp.int32, (rows, span), 0)
    key_pos = scalars[3] + lax.broadcasted_iota(jnp.int32, (rows, span), 1)
    allowed = (
        (key_pos <= query_pos)
        & (key_pos > query_pos - WINDOW)
        & (key_pos >= 0)
        & (key_pos < seq_len)
    )
    bias_ref[...] = jnp.where(allowed, 0.0, neg_floor)
    if nparts == 1:
        k = part_refs[0][0, pl.ds(key_start, span), :]
        v = part_refs[0][1, pl.ds(key_start, span), :]
    else:
        k = jnp.concatenate([p[0] for p in part_refs], axis=0)
        v = jnp.concatenate([p[1] for p in part_refs], axis=0)
    if slots:
        slot_pos = scalars[4] + lax.broadcasted_iota(jnp.int32, (slots, span), 0)
        held_pos = scalars[3] + lax.broadcasted_iota(jnp.int32, (slots, span), 1)
        pick = ((held_pos == slot_pos) & (slot_pos >= 0)).astype(jnp.bfloat16)
        cache_ref[0] = jnp.dot(pick, k, preferred_element_type=jnp.float32).astype(cache_ref.dtype)
        cache_ref[1] = jnp.dot(pick, v, preferred_element_type=jnp.float32).astype(cache_ref.dtype)
    batch = 4 if group % 4 == 0 else 1
    valid = (first_pos + lax.broadcasted_iota(jnp.int32, (batch, rows, 1), 1)) < seq_len
    valid = valid.reshape(batch * rows, 1)
    scale = 1.0 / math.sqrt(HD)
    for lead in range(0, group, batch):
        heads = slice(lead * rows, (lead + batch) * rows)
        raw = lax.dot_general(
            q_ref[0, heads, :], k, (((1,), (1,)), ((), ())), preferred_element_type=jnp.float32
        )
        raw = (raw.reshape(batch, rows, span) + bias_ref[...][None]).reshape(batch * rows, span)
        row_top = jnp.max(raw, axis=-1, keepdims=True)
        weights = jnp.exp((raw - row_top) * scale)
        totals = jnp.sum(weights, axis=-1, keepdims=True)
        numer = jnp.dot(weights.astype(jnp.bfloat16), v, preferred_element_type=jnp.float32)
        denom = jnp.where(valid, totals, 1.0)
        o_ref[0, heads, :] = jnp.where(valid, numer / denom, 0.0).astype(o_ref.dtype)


def attention(scalars, rotated_q, parts, kv_heads_dev, group_size, span, slots):
    rows = rotated_q.shape[1] // group_size
    nparts = len(parts)
    kernel = functools.partial(
        attend_kernel, rows=rows, span=span, group=group_size, nparts=nparts, slots=slots
    )
    width = group_size * HD
    out_specs = pl.BlockSpec((1, group_size * rows, HD), lambda j, s: (j, 0, 0))
    out_shape = jax.ShapeDtypeStruct((kv_heads_dev, group_size * rows, HD), jnp.bfloat16)
    if slots:
        out_specs = [out_specs, pl.BlockSpec((2, slots, HD), lambda j, s: (0, 0, j))]
        out_shape = [
            out_shape,
            jax.ShapeDtypeStruct((2, slots, kv_heads_dev * HD), jnp.bfloat16),
        ]
    grid_spec = pltpu.PrefetchScalarGridSpec(
        num_scalar_prefetch=1,
        grid=(kv_heads_dev,),
        in_specs=[pl.BlockSpec((1, group_size * rows, HD), lambda j, s: (j, 0, 0))]
        + [pl.BlockSpec((2, p.shape[1], HD), lambda j, s: (0, 0, j)) for p in parts],
        out_specs=out_specs,
        scratch_shapes=[pltpu.VMEM((rows, span), jnp.float32)],
    )
    return pl.pallas_call(kernel, grid_spec=grid_spec, out_shape=out_shape)(
        scalars, rotated_q, *parts
    )


def passed_along(x, by):
    devices = lax.axis_size("seq")
    pairs = [(i, i + by) for i in range(devices) if 0 <= i + by < devices]
    return lax.ppermute(x, "seq", pairs)


def local(queries, keys_values, lengths):
    seq_len = lengths[0]
    shard_rows = queries.shape[1]
    width = keys_values.shape[-1]
    kv_heads_dev = width // HD
    heads_dev = queries.shape[-1] // HD
    group_size = heads_dev // kv_heads_dev
    seq_index = lax.axis_index("seq")
    seq_count = lax.axis_size("seq")
    tokens = seq_count * shard_rows
    first_pos = seq_index * shard_rows
    positions = first_pos + jnp.arange(shard_rows, dtype=jnp.int32)
    rotated_q = rotate(queries[0].reshape(shard_rows, heads_dev, HD).astype(jnp.float32), positions)
    rotated_q = (
        rotated_q.astype(jnp.bfloat16)
        .reshape(shard_rows, kv_heads_dev, group_size, HD)
        .transpose(1, 2, 0, 3)
        .reshape(kv_heads_dev, group_size * shard_rows, HD)
    )
    rotated_k = rotate(
        keys_values[0, 0].reshape(shard_rows, kv_heads_dev, HD).astype(jnp.float32), positions
    )
    own_block = jnp.stack(
        [rotated_k.astype(jnp.bfloat16).reshape(shard_rows, width), keys_values[0, 1]]
    )
    reach_count = min(WINDOW // shard_rows, seq_count - 1)
    span = (reach_count + 1) * shard_rows
    slot_rows = WINDOW // seq_count
    if WINDOW >= tokens:
        shifted = [own_block]
        for hop in range(1, reach_count + 1):
            shifted.insert(0, passed_along(own_block, hop))
        parts = shifted
        key_index = jnp.zeros((), jnp.int32)
        key_first = first_pos - reach_count * shard_rows
    else:
        outbox = jnp.broadcast_to(own_block[:, None], (2, seq_count, shard_rows, width))
        held = lax.all_to_all(
            outbox.reshape(2, tokens, width), "seq", 1, 1, tiled=True
        )
        parts = [held]
        held_first = 0
        key_index = jnp.maximum(first_pos - reach_count * shard_rows, 0)
        key_first = key_index
    slot_first = seq_len - WINDOW + seq_index * slot_rows
    scalars = jnp.stack([seq_len, first_pos, key_index, key_first, slot_first]).astype(jnp.int32)
    if WINDOW >= tokens:
        attended, window_cache = attention(
            scalars, rotated_q, parts, kv_heads_dev, group_size, span, slot_rows
        )
    else:
        attended = attention(scalars, rotated_q, parts, kv_heads_dev, group_size, span, 0)
        padded = jnp.concatenate([jnp.zeros((2, slot_rows, width), jnp.bfloat16), held], axis=1)
        begin_row = slot_first - held_first + slot_rows
        window_cache = lax.dynamic_slice_in_dim(padded, jnp.maximum(begin_row, 0), slot_rows, 1)
    attended = (
        attended.reshape(kv_heads_dev, group_size, shard_rows, HD)
        .transpose(2, 0, 1, 3)
        .reshape(1, shard_rows, heads_dev * HD)
    )
    return (attended, window_cache[None])


def solution(mesh):
    return jax.shard_map(
        local,
        mesh=mesh,
        in_specs=(
            P("section", ("parts", "seq"), "tp"),
            P("section", None, ("parts", "seq"), "tp"),
            P("parts"),
        ),
        out_specs=(
            P("section", ("parts", "seq"), "tp"),
            P("section", None, ("parts", "seq"), "tp"),
        ),
        check_vma=False,
    )
```

```python
import functools
import math

import jax
import jax.numpy as jnp
from jax import lax
from jax.experimental import pallas as pl
from jax.experimental.pallas import tpu as pltpu
from jax.sharding import PartitionSpec as P

HD = 128
WINDOW = 2048


rope_base = 1000000.0
neg_floor = -1e30


def rotate(field, positions):
    half_dim = field.shape[-1] // 2
    frequency = jnp.exp(
        jnp.arange(half_dim, dtype=jnp.float32) * (-2.0 * math.log(rope_base) / field.shape[-1])
    )
    angles = positions.astype(jnp.float32)[:, None] * frequency[None, :]
    cosine = jnp.cos(angles)[:, None, :]
    sine_part = jnp.sin(angles)[:, None, :]
    lower_half = field[..., :half_dim]
    upper_half = field[..., half_dim:]
    return jnp.concatenate(
        [
            lower_half * cosine - upper_half * sine_part,
            upper_half * cosine + lower_half * sine_part,
        ],
        axis=-1,
    )


def attend_kernel(scalars, q_ref, *refs, rows, span, group, nparts, slots):
    part_refs = refs[:nparts]
    if slots:
        o_ref, cache_ref, bias_ref, pick_ref = refs[nparts:]
    else:
        o_ref, bias_ref = refs[nparts:]
    seq_len = scalars[0]
    first_pos = scalars[1]
    key_start = pl.multiple_of(scalars[2], 256)
    query_pos = first_pos + lax.broadcasted_iota(jnp.int32, (rows, span), 0)
    key_pos = scalars[3] + lax.broadcasted_iota(jnp.int32, (rows, span), 1)
    allowed = (
        (key_pos <= query_pos)
        & (key_pos > query_pos - WINDOW)
        & (key_pos >= 0)
        & (key_pos < seq_len)
    )

    @pl.when(pl.program_id(0) == 0)
    def _():
        bias_ref[...] = jnp.where(allowed, 0.0, neg_floor)
        if slots:
            slot_pos = scalars[4] + lax.broadcasted_iota(jnp.int32, (slots, span), 0)
            held_pos = scalars[3] + lax.broadcasted_iota(jnp.int32, (slots, span), 1)
            pick_ref[...] = ((held_pos == slot_pos) & (slot_pos >= 0)).astype(jnp.bfloat16)

    if nparts == 1:
        k = part_refs[0][0, pl.ds(key_start, span), :]
        v = part_refs[0][1, pl.ds(key_start, span), :]
    else:
        k = jnp.concatenate([p[0] for p in part_refs], axis=0)
        v = jnp.concatenate([p[1] for p in part_refs], axis=0)
    if slots:
        pick = pick_ref[...]
        cache_ref[0] = jnp.dot(pick, k, preferred_element_type=jnp.float32).astype(cache_ref.dtype)
        cache_ref[1] = jnp.dot(pick, v, preferred_element_type=jnp.float32).astype(cache_ref.dtype)
    valid = (first_pos + lax.broadcasted_iota(jnp.int32, (rows, 1), 0)) < seq_len
    scale = 1.0 / math.sqrt(HD)
    for head in range(group):
        cols = slice(head * HD, (head + 1) * HD)
        raw = lax.dot_general(
            q_ref[:, cols], k, (((1,), (1,)), ((), ())), preferred_element_type=jnp.float32
        ) + bias_ref[...]
        row_top = jnp.max(raw, axis=-1, keepdims=True)
        weights = jnp.exp((raw - row_top) * scale)
        totals = jnp.sum(weights, axis=-1, keepdims=True)
        numer = jnp.dot(weights.astype(jnp.bfloat16), v, preferred_element_type=jnp.float32)
        denom = jnp.where(valid, totals, 1.0)
        o_ref[:, cols] = jnp.where(valid, numer / denom, 0.0).astype(o_ref.dtype)


def attention(scalars, rotated_q, parts, kv_heads_dev, group_size, span, slots):
    rows = rotated_q.shape[0]
    nparts = len(parts)
    kernel = functools.partial(
        attend_kernel, rows=rows, span=span, group=group_size, nparts=nparts, slots=slots
    )
    width = group_size * HD
    out_specs = pl.BlockSpec((rows, width), lambda j, s: (0, j))
    out_shape = jax.ShapeDtypeStruct((rows, kv_heads_dev * width), jnp.bfloat16)
    if slots:
        out_specs = [out_specs, pl.BlockSpec((2, slots, HD), lambda j, s: (0, 0, j))]
        out_shape = [
            out_shape,
            jax.ShapeDtypeStruct((2, slots, kv_heads_dev * HD), jnp.bfloat16),
        ]
    grid_spec = pltpu.PrefetchScalarGridSpec(
        num_scalar_prefetch=1,
        grid=(kv_heads_dev,),
        in_specs=[pl.BlockSpec((rows, width), lambda j, s: (0, j))]
        + [pl.BlockSpec((2, p.shape[1], HD), lambda j, s: (0, 0, j)) for p in parts],
        out_specs=out_specs,
        scratch_shapes=[pltpu.VMEM((rows, span), jnp.float32)]
        + ([pltpu.VMEM((slots, span), jnp.bfloat16)] if slots else []),
    )
    return pl.pallas_call(kernel, grid_spec=grid_spec, out_shape=out_shape)(
        scalars, rotated_q, *parts
    )


def passed_along(x, by):
    devices = lax.axis_size("seq")
    pairs = [(i, i + by) for i in range(devices) if 0 <= i + by < devices]
    return lax.ppermute(x, "seq", pairs)


def local(queries, keys_values, lengths):
    seq_len = lengths[0]
    shard_rows = queries.shape[1]
    width = keys_values.shape[-1]
    kv_heads_dev = width // HD
    heads_dev = queries.shape[-1] // HD
    group_size = heads_dev // kv_heads_dev
    seq_index = lax.axis_index("seq")
    seq_count = lax.axis_size("seq")
    tokens = seq_count * shard_rows
    first_pos = seq_index * shard_rows
    positions = first_pos + jnp.arange(shard_rows, dtype=jnp.int32)
    rotated_q = rotate(queries[0].reshape(shard_rows, heads_dev, HD).astype(jnp.float32), positions)
    rotated_q = rotated_q.astype(jnp.bfloat16).reshape(shard_rows, heads_dev * HD)
    rotated_k = rotate(
        keys_values[0, 0].reshape(shard_rows, kv_heads_dev, HD).astype(jnp.float32), positions
    )
    own_block = jnp.stack(
        [rotated_k.astype(jnp.bfloat16).reshape(shard_rows, width), keys_values[0, 1]]
    )
    reach_count = min(WINDOW // shard_rows, seq_count - 1)
    span = (reach_count + 1) * shard_rows
    slot_rows = WINDOW // seq_count
    if WINDOW >= tokens:
        shifted = [own_block]
        for hop in range(1, reach_count + 1):
            shifted.insert(0, passed_along(own_block, hop))
        parts = shifted
        key_index = jnp.zeros((), jnp.int32)
        key_first = first_pos - reach_count * shard_rows
    else:
        outbox = jnp.broadcast_to(own_block[:, None], (2, seq_count, shard_rows, width))
        held = lax.all_to_all(
            outbox.reshape(2, tokens, width), "seq", 1, 1, tiled=True
        )
        parts = [held]
        held_first = 0
        key_index = jnp.maximum(first_pos - reach_count * shard_rows, 0)
        key_first = key_index
    slot_first = seq_len - WINDOW + seq_index * slot_rows
    scalars = jnp.stack([seq_len, first_pos, key_index, key_first, slot_first]).astype(jnp.int32)
    if WINDOW >= tokens:
        attended, window_cache = attention(
            scalars, rotated_q, parts, kv_heads_dev, group_size, span, slot_rows
        )
    else:
        attended = attention(scalars, rotated_q, parts, kv_heads_dev, group_size, span, 0)
        padded = jnp.concatenate([jnp.zeros((2, slot_rows, width), jnp.bfloat16), held], axis=1)
        begin_row = slot_first - held_first + slot_rows
        window_cache = lax.dynamic_slice_in_dim(padded, jnp.maximum(begin_row, 0), slot_rows, 1)
    attended = attended.reshape(1, shard_rows, heads_dev * HD)
    return (attended, window_cache[None])


def solution(mesh):
    return jax.shard_map(
        local,
        mesh=mesh,
        in_specs=(
            P("section", ("parts", "seq"), "tp"),
            P("section", None, ("parts", "seq"), "tp"),
            P("parts"),
        ),
        out_specs=(
            P("section", ("parts", "seq"), "tp"),
            P("section", None, ("parts", "seq"), "tp"),
        ),
        check_vma=False,
    )
```

```python
import functools
import math

import jax
import jax.numpy as jnp
from jax import lax
from jax.experimental import pallas as pl
from jax.experimental.pallas import tpu as pltpu
from jax.sharding import PartitionSpec as P

HD = 128
WINDOW = 2048


rope_base = 1000000.0
neg_floor = -1e30


def rotate(field, positions):
    half_dim = field.shape[-1] // 2
    frequency = jnp.exp(
        jnp.arange(half_dim, dtype=jnp.float32) * (-2.0 * math.log(rope_base) / field.shape[-1])
    )
    angles = positions.astype(jnp.float32)[:, None] * frequency[None, :]
    cosine = jnp.cos(angles)[:, None, :]
    sine_part = jnp.sin(angles)[:, None, :]
    lower_half = field[..., :half_dim]
    upper_half = field[..., half_dim:]
    return jnp.concatenate(
        [
            lower_half * cosine - upper_half * sine_part,
            upper_half * cosine + lower_half * sine_part,
        ],
        axis=-1,
    )


def attend_kernel(scalars, q_ref, *refs, rows, span, group, nparts, slots):
    part_refs = refs[:nparts]
    if slots:
        o_ref, cache_ref, bias_ref = refs[nparts:]
    else:
        o_ref, bias_ref = refs[nparts:]
    seq_len = scalars[0]
    first_pos = scalars[1]
    key_start = pl.multiple_of(scalars[2], 256)
    query_pos = first_pos + lax.broadcasted_iota(jnp.int32, (rows, span), 0)
    key_pos = scalars[3] + lax.broadcasted_iota(jnp.int32, (rows, span), 1)
    allowed = (
        (key_pos <= query_pos)
        & (key_pos > query_pos - WINDOW)
        & (key_pos >= 0)
        & (key_pos < seq_len)
    )
    bias_ref[...] = jnp.where(allowed, 0.0, neg_floor)
    col = pl.ds(pl.multiple_of(pl.program_id(0) * HD, HD), HD)
    if nparts == 1:
        k = part_refs[0][0, pl.ds(key_start, span), col]
        v = part_refs[0][1, pl.ds(key_start, span), col]
    else:
        k = jnp.concatenate([p[0, :, col] for p in part_refs], axis=0)
        v = jnp.concatenate([p[1, :, col] for p in part_refs], axis=0)
    if slots:
        slot_pos = scalars[4] + lax.broadcasted_iota(jnp.int32, (slots, span), 0)
        held_pos = scalars[3] + lax.broadcasted_iota(jnp.int32, (slots, span), 1)
        pick = ((held_pos == slot_pos) & (slot_pos >= 0)).astype(jnp.bfloat16)
        cache_ref[0] = jnp.dot(pick, k, preferred_element_type=jnp.float32).astype(cache_ref.dtype)
        cache_ref[1] = jnp.dot(pick, v, preferred_element_type=jnp.float32).astype(cache_ref.dtype)
    valid = (first_pos + lax.broadcasted_iota(jnp.int32, (rows, 1), 0)) < seq_len
    scale = 1.0 / math.sqrt(HD)
    for head in range(group):
        cols = slice(head * HD, (head + 1) * HD)
        raw = lax.dot_general(
            q_ref[:, cols], k, (((1,), (1,)), ((), ())), preferred_element_type=jnp.float32
        ) + bias_ref[...]
        row_top = jnp.max(raw, axis=-1, keepdims=True)
        weights = jnp.exp((raw - row_top) * scale)
        totals = jnp.sum(weights, axis=-1, keepdims=True)
        numer = jnp.dot(weights.astype(jnp.bfloat16), v, preferred_element_type=jnp.float32)
        denom = jnp.where(valid, totals, 1.0)
        o_ref[:, cols] = jnp.where(valid, numer / denom, 0.0).astype(o_ref.dtype)


def attention(scalars, rotated_q, parts, kv_heads_dev, group_size, span, slots):
    rows = rotated_q.shape[0]
    nparts = len(parts)
    kernel = functools.partial(
        attend_kernel, rows=rows, span=span, group=group_size, nparts=nparts, slots=slots
    )
    width = group_size * HD
    out_specs = pl.BlockSpec((rows, width), lambda j, s: (0, j))
    out_shape = jax.ShapeDtypeStruct((rows, kv_heads_dev * width), jnp.bfloat16)
    if slots:
        out_specs = [out_specs, pl.BlockSpec((2, slots, HD), lambda j, s: (0, 0, j))]
        out_shape = [
            out_shape,
            jax.ShapeDtypeStruct((2, slots, kv_heads_dev * HD), jnp.bfloat16),
        ]
    grid_spec = pltpu.PrefetchScalarGridSpec(
        num_scalar_prefetch=1,
        grid=(kv_heads_dev,),
        in_specs=[pl.BlockSpec((rows, width), lambda j, s: (0, j))]
        + [pl.BlockSpec(memory_space=pltpu.VMEM) for p in parts],
        out_specs=out_specs,
        scratch_shapes=[pltpu.VMEM((rows, span), jnp.float32)],
    )
    return pl.pallas_call(kernel, grid_spec=grid_spec, out_shape=out_shape)(
        scalars, rotated_q, *parts
    )


def passed_along(x, by):
    devices = lax.axis_size("seq")
    pairs = [(i, i + by) for i in range(devices) if 0 <= i + by < devices]
    return lax.ppermute(x, "seq", pairs)


def local(queries, keys_values, lengths):
    seq_len = lengths[0]
    shard_rows = queries.shape[1]
    width = keys_values.shape[-1]
    kv_heads_dev = width // HD
    heads_dev = queries.shape[-1] // HD
    group_size = heads_dev // kv_heads_dev
    seq_index = lax.axis_index("seq")
    seq_count = lax.axis_size("seq")
    tokens = seq_count * shard_rows
    first_pos = seq_index * shard_rows
    positions = first_pos + jnp.arange(shard_rows, dtype=jnp.int32)
    rotated_q = rotate(queries[0].reshape(shard_rows, heads_dev, HD).astype(jnp.float32), positions)
    rotated_q = rotated_q.astype(jnp.bfloat16).reshape(shard_rows, heads_dev * HD)
    rotated_k = rotate(
        keys_values[0, 0].reshape(shard_rows, kv_heads_dev, HD).astype(jnp.float32), positions
    )
    own_block = jnp.stack(
        [rotated_k.astype(jnp.bfloat16).reshape(shard_rows, width), keys_values[0, 1]]
    )
    reach_count = min(WINDOW // shard_rows, seq_count - 1)
    span = (reach_count + 1) * shard_rows
    slot_rows = WINDOW // seq_count
    if WINDOW >= tokens:
        shifted = [own_block]
        for hop in range(1, reach_count + 1):
            shifted.insert(0, passed_along(own_block, hop))
        parts = shifted
        key_index = jnp.zeros((), jnp.int32)
        key_first = first_pos - reach_count * shard_rows
    else:
        outbox = jnp.broadcast_to(own_block[:, None], (2, seq_count, shard_rows, width))
        held = lax.all_to_all(
            outbox.reshape(2, tokens, width), "seq", 1, 1, tiled=True
        )
        parts = [held]
        held_first = 0
        key_index = jnp.maximum(first_pos - reach_count * shard_rows, 0)
        key_first = key_index
    slot_first = seq_len - WINDOW + seq_index * slot_rows
    scalars = jnp.stack([seq_len, first_pos, key_index, key_first, slot_first]).astype(jnp.int32)
    if WINDOW >= tokens:
        attended, window_cache = attention(
            scalars, rotated_q, parts, kv_heads_dev, group_size, span, slot_rows
        )
    else:
        attended = attention(scalars, rotated_q, parts, kv_heads_dev, group_size, span, 0)
        padded = jnp.concatenate([jnp.zeros((2, slot_rows, width), jnp.bfloat16), held], axis=1)
        begin_row = slot_first - held_first + slot_rows
        window_cache = lax.dynamic_slice_in_dim(padded, jnp.maximum(begin_row, 0), slot_rows, 1)
    attended = attended.reshape(1, shard_rows, heads_dev * HD)
    return (attended, window_cache[None])


def solution(mesh):
    return jax.shard_map(
        local,
        mesh=mesh,
        in_specs=(
            P("section", ("parts", "seq"), "tp"),
            P("section", None, ("parts", "seq"), "tp"),
            P("parts"),
        ),
        out_specs=(
            P("section", ("parts", "seq"), "tp"),
            P("section", None, ("parts", "seq"), "tp"),
        ),
        check_vma=False,
    )
```

```python
import functools
import math

import jax
import jax.numpy as jnp
from jax import lax
from jax.experimental import pallas as pl
from jax.experimental.pallas import tpu as pltpu
from jax.sharding import PartitionSpec as P

HD = 128
WINDOW = 2048


rope_base = 1000000.0
neg_floor = -1e30


def rotate(field, positions):
    half_dim = field.shape[-1] // 2
    frequency = jnp.exp(
        jnp.arange(half_dim, dtype=jnp.float32) * (-2.0 * math.log(rope_base) / field.shape[-1])
    )
    angles = positions.astype(jnp.float32)[:, None] * frequency[None, :]
    cosine = jnp.cos(angles)[:, None, :]
    sine_part = jnp.sin(angles)[:, None, :]
    lower_half = field[..., :half_dim]
    upper_half = field[..., half_dim:]
    return jnp.concatenate(
        [
            lower_half * cosine - upper_half * sine_part,
            upper_half * cosine + lower_half * sine_part,
        ],
        axis=-1,
    )


def attend_kernel(scalars, q_ref, *refs, rows, span, group, nparts, slots):
    part_refs = refs[:nparts]
    if slots:
        o_ref, cache_ref, bias_ref = refs[nparts:]
    else:
        o_ref, bias_ref = refs[nparts:]
    seq_len = scalars[0]
    first_pos = scalars[1]
    key_start = pl.multiple_of(scalars[2], 256)
    query_pos = first_pos + lax.broadcasted_iota(jnp.int32, (rows, span), 0)
    key_pos = scalars[3] + lax.broadcasted_iota(jnp.int32, (rows, span), 1)
    allowed = (
        (key_pos <= query_pos)
        & (key_pos > query_pos - WINDOW)
        & (key_pos >= 0)
        & (key_pos < seq_len)
    )
    bias_ref[...] = jnp.where(allowed, 0.0, neg_floor)
    if nparts == 1:
        k = part_refs[0][0, pl.ds(key_start, span), :]
        v = part_refs[0][1, pl.ds(key_start, span), :]
    else:
        k = jnp.concatenate([p[0] for p in part_refs], axis=0)
        v = jnp.concatenate([p[1] for p in part_refs], axis=0)
    if slots:
        slot_pos = scalars[4] + lax.broadcasted_iota(jnp.int32, (slots, span), 0)
        held_pos = scalars[3] + lax.broadcasted_iota(jnp.int32, (slots, span), 1)
        pick = ((held_pos == slot_pos) & (slot_pos >= 0)).astype(jnp.bfloat16)
        cache_ref[0] = jnp.dot(pick, k, preferred_element_type=jnp.float32).astype(cache_ref.dtype)
        cache_ref[1] = jnp.dot(pick, v, preferred_element_type=jnp.float32).astype(cache_ref.dtype)
    valid = (first_pos + lax.broadcasted_iota(jnp.int32, (rows, 1), 0)) < seq_len
    scale = 1.0 / math.sqrt(HD)
    for head in range(group):
        cols = slice(head * HD, (head + 1) * HD)
        raw = lax.dot_general(
            q_ref[:, cols], k, (((1,), (1,)), ((), ())), preferred_element_type=jnp.float32
        ) + bias_ref[...]
        row_top = jnp.max(raw, axis=-1, keepdims=True)
        weights = jnp.exp((raw - row_top) * scale)
        totals = jnp.sum(weights, axis=-1, keepdims=True)
        numer = jnp.dot(weights.astype(jnp.bfloat16), v, preferred_element_type=jnp.float32)
        inverse = jnp.where(valid, 1.0 / jnp.where(valid, totals, 1.0), 0.0)
        o_ref[:, cols] = (numer * inverse).astype(o_ref.dtype)


def attention(scalars, rotated_q, parts, kv_heads_dev, group_size, span, slots):
    rows = rotated_q.shape[0]
    nparts = len(parts)
    kernel = functools.partial(
        attend_kernel, rows=rows, span=span, group=group_size, nparts=nparts, slots=slots
    )
    width = group_size * HD
    out_specs = pl.BlockSpec((rows, width), lambda j, s: (0, j))
    out_shape = jax.ShapeDtypeStruct((rows, kv_heads_dev * width), jnp.bfloat16)
    if slots:
        out_specs = [out_specs, pl.BlockSpec((2, slots, HD), lambda j, s: (0, 0, j))]
        out_shape = [
            out_shape,
            jax.ShapeDtypeStruct((2, slots, kv_heads_dev * HD), jnp.bfloat16),
        ]
    grid_spec = pltpu.PrefetchScalarGridSpec(
        num_scalar_prefetch=1,
        grid=(kv_heads_dev,),
        in_specs=[pl.BlockSpec((rows, width), lambda j, s: (0, j))]
        + [pl.BlockSpec((2, p.shape[1], HD), lambda j, s: (0, 0, j)) for p in parts],
        out_specs=out_specs,
        scratch_shapes=[pltpu.VMEM((rows, span), jnp.float32)],
    )
    return pl.pallas_call(kernel, grid_spec=grid_spec, out_shape=out_shape)(
        scalars, rotated_q, *parts
    )


def passed_along(x, by):
    devices = lax.axis_size("seq")
    pairs = [(i, i + by) for i in range(devices) if 0 <= i + by < devices]
    return lax.ppermute(x, "seq", pairs)


def local(queries, keys_values, lengths):
    seq_len = lengths[0]
    shard_rows = queries.shape[1]
    width = keys_values.shape[-1]
    kv_heads_dev = width // HD
    heads_dev = queries.shape[-1] // HD
    group_size = heads_dev // kv_heads_dev
    seq_index = lax.axis_index("seq")
    seq_count = lax.axis_size("seq")
    tokens = seq_count * shard_rows
    first_pos = seq_index * shard_rows
    positions = first_pos + jnp.arange(shard_rows, dtype=jnp.int32)
    rotated_q = rotate(queries[0].reshape(shard_rows, heads_dev, HD).astype(jnp.float32), positions)
    rotated_q = rotated_q.astype(jnp.bfloat16).reshape(shard_rows, heads_dev * HD)
    rotated_k = rotate(
        keys_values[0, 0].reshape(shard_rows, kv_heads_dev, HD).astype(jnp.float32), positions
    )
    own_block = jnp.stack(
        [rotated_k.astype(jnp.bfloat16).reshape(shard_rows, width), keys_values[0, 1]]
    )
    reach_count = min(WINDOW // shard_rows, seq_count - 1)
    span = (reach_count + 1) * shard_rows
    slot_rows = WINDOW // seq_count
    if WINDOW >= tokens:
        shifted = [own_block]
        for hop in range(1, reach_count + 1):
            shifted.insert(0, passed_along(own_block, hop))
        parts = shifted
        key_index = jnp.zeros((), jnp.int32)
        key_first = first_pos - reach_count * shard_rows
    else:
        outbox = jnp.broadcast_to(own_block[:, None], (2, seq_count, shard_rows, width))
        held = lax.all_to_all(
            outbox.reshape(2, tokens, width), "seq", 1, 1, tiled=True
        )
        parts = [held]
        held_first = 0
        key_index = jnp.maximum(first_pos - reach_count * shard_rows, 0)
        key_first = key_index
    slot_first = seq_len - WINDOW + seq_index * slot_rows
    scalars = jnp.stack([seq_len, first_pos, key_index, key_first, slot_first]).astype(jnp.int32)
    if WINDOW >= tokens:
        attended, window_cache = attention(
            scalars, rotated_q, parts, kv_heads_dev, group_size, span, slot_rows
        )
    else:
        attended = attention(scalars, rotated_q, parts, kv_heads_dev, group_size, span, 0)
        padded = jnp.concatenate([jnp.zeros((2, slot_rows, width), jnp.bfloat16), held], axis=1)
        begin_row = slot_first - held_first + slot_rows
        window_cache = lax.dynamic_slice_in_dim(padded, jnp.maximum(begin_row, 0), slot_rows, 1)
    attended = attended.reshape(1, shard_rows, heads_dev * HD)
    return (attended, window_cache[None])


def solution(mesh):
    return jax.shard_map(
        local,
        mesh=mesh,
        in_specs=(
            P("section", ("parts", "seq"), "tp"),
            P("section", None, ("parts", "seq"), "tp"),
            P("parts"),
        ),
        out_specs=(
            P("section", ("parts", "seq"), "tp"),
            P("section", None, ("parts", "seq"), "tp"),
        ),
        check_vma=False,
    )
```
